512 devices in a mesh: samp: 64 (over z, x, core), feat: 8 (over y).
Axes of the slice: x: 4, y: 8, z: 8, core: 2. Of those that a mesh axis runs over, the one named last changes fastest.
Arguments:
- images: bfloat16 [8192, 4096], P('samp', 'feat')
- labels: int32 [8192], P('samp'), may hold values from 0 to 12287, as said below
- owner: int32 [12288], replicated, may hold values from 0 to 63, as said below
- basis: bfloat16 [4096, 512], P('feat'), may hold values from -5 to 5
Outputs:
- owner_means: bfloat16 [12288, 4096], P('samp', 'feat')
- within: float32 [512, 4096], P('samp', 'feat')
- between: float32 [512, 4096], P('samp', 'feat')
The draws below stay inside these ranges and needn't reach their ends.
Inputs may be any that keep to these rules, and one draw needn't show every extreme that they name: Each owner index holds exactly 192 classes. `labels`: in each aligned block of 128 images, at most 4 images have classes of one owner; one owner receives exactly 4 from every block.
All inputs are finite; a program needn't handle non-finite values.
Results may differ from the reference program's by a relative error of at most 0.0095.
Values may be sent and summed in bfloat16 or wider, within the bound.
No kernel may reach another device: no remote copies, remote signals or barrier semaphores. Data moves between devices by JAX's collectives and lax.ppermute only.
A program may use at most 64 MiB of HBM per device.

```python
import jax
import jax.numpy as jnp

F = 4096
K = 512
CLS_DEV = 192
TOK_DEV = 128
CLASSES = 12288
TOKENS = 8192
CAP = 4


def tables(key):
    shuffle = jax.random.permutation(jax.random.fold_in(key, 101), CLASSES)
    return ((shuffle // CLS_DEV).astype(jnp.int32), jnp.argsort(shuffle).astype(jnp.int32))


def draw_owner(key, part):
    return tables(key)[0]


def draw_labels(key, part):
    blocks = TOKENS // TOK_DEV
    heavy_count = blocks // 4
    owners_of, inverse = tables(key)
    favoured = jax.random.randint(jax.random.fold_in(key, 102), (), 0, blocks)
    positions = jnp.arange(TOK_DEV)
    chosen = jnp.where(positions < heavy_count * CAP, positions // CAP, heavy_count + (positions - heavy_count * CAP) % (blocks - heavy_count))

    def one_block(block_key):
        key_one, key_two, key_three = jax.random.split(block_key, 3)
        ranking = jax.random.permutation(key_one, blocks)
        head_owner = ranking[0]
        ranking = jnp.where(ranking == favoured, head_owner, ranking).at[0].set(favoured)
        target = ranking[chosen]
        target = target[jax.random.permutation(key_two, TOK_DEV)]
        within_owner = jax.random.randint(key_three, (TOK_DEV,), 0, CLS_DEV)
        return inverse[target * CLS_DEV + within_owner]
    block_keys = jax.random.split(jax.random.fold_in(key, 103), blocks)
    return jax.vmap(one_block)(block_keys).reshape(-1).astype(jnp.int32)


def draw_images(key, part):
    blocks = TOKENS // TOK_DEV
    key_one, key_two = jax.random.split(jax.random.fold_in(key, 104), 2)
    growth = 1.0 + 2.0 * (jnp.arange(TOKENS) // TOK_DEV).astype(jnp.float32) / max(blocks - 1, 1)
    offset = jax.random.uniform(key_two, (F,), jnp.float32, -1.0, 1.0)
    jitter = jax.random.normal(key_one, (TOKENS, F), jnp.float32)
    return (offset[None, :] + jitter * growth[:, None]).astype(jnp.bfloat16)


def shard_levels(own_key, extent, pieces, smallest, largest):
    factor_of = 1.0
    for dim, shards_of in pieces:
        heights = jax.random.uniform(jax.random.fold_in(jax.random.fold_in(own_key, 6), dim), (shards_of,), jnp.float32, smallest / len(pieces), largest / len(pieces))
        factor_of = factor_of * jnp.repeat(jnp.exp(heights), extent[dim] // shards_of).reshape((-1,) + (1,) * (len(extent) - 1 - dim))
    return factor_of


def bell_draw(stream_key, dims, scale, most, pieces=(), kind=jnp.bfloat16):
    array = jax.random.normal(stream_key, dims, jnp.float32) * scale
    if len(pieces) > 0:
        array = shard_levels(stream_key, dims, pieces, -0.22, 0.18) * array
    return jnp.clip(array, min=-most, max=most).astype(kind)


def setup_inputs(seed: int = 0) -> dict:
    key_list = jax.random.split(jax.random.key(seed), 5)
    return {
        "images": draw_images(jax.random.fold_in(key_list[4], 71), 0),
        "labels": draw_labels(jax.random.fold_in(key_list[4], 71), 0),
        "owner": draw_owner(jax.random.fold_in(key_list[4], 71), 0),
        "basis": bell_draw(key_list[3], (F, K), 1.0, 5.0, ((0, 8),)),
    }


def reference(images, labels, owner, basis):
    as_float = images.astype(jnp.float32)
    class_sums = jax.ops.segment_sum(as_float, labels, num_segments=CLASSES)
    counts = jax.ops.segment_sum(jnp.ones(labels.shape, jnp.float32), labels, num_segments=CLASSES)
    class_means = class_sums / jnp.maximum(counts, 1.0)[:, None]
    center = jnp.sum(as_float, axis=0) / TOKENS
    by_owner = jnp.argsort(owner, stable=True)
    owner_means = class_means[by_owner].astype(jnp.bfloat16)
    centred = (as_float - class_means[labels]).astype(jnp.bfloat16)
    deviation = (class_means - center[None, :]).astype(jnp.bfloat16)
    projected = jnp.dot(centred, basis, preferred_element_type=jnp.float32).astype(jnp.bfloat16)
    weighted = (counts[:, None] * jnp.dot(deviation, basis, preferred_element_type=jnp.float32)).astype(jnp.bfloat16)
    within = jnp.dot(projected.T, centred, preferred_element_type=jnp.float32) / TOKENS
    between = jnp.dot(weighted.T, deviation, preferred_element_type=jnp.float32) / TOKENS
    return owner_means, within, between
```

```python
import jax
import jax.numpy as jnp
from jax import lax
from jax.sharding import PartitionSpec as P

CLS_DEV = 192


def on_device(images, labels, owner, basis):
    samp_count = lax.axis_size("samp")
    row_count, feat_width = images.shape
    slot_cap = 2 * row_count // samp_count
    class_cap = CLS_DEV
    class_total = owner.shape[0]
    k_width = basis.shape[1]
    target = jnp.take(owner, labels)
    onehot_dest = (target[:, None] == jnp.arange(samp_count)[None, :]).astype(jnp.int32)
    slot_index = jnp.sum(jnp.cumsum(onehot_dest, axis=0) * onehot_dest, axis=1) - 1
    position = target * slot_cap + slot_index
    same_owner = owner[None, :] == target[:, None]
    earlier = jnp.arange(class_total)[None, :] < labels[:, None]
    slot_ids = jnp.sum((same_owner & earlier).astype(jnp.int32), axis=1)
    send_rows = (
        jnp.zeros((samp_count * slot_cap, feat_width), jnp.bfloat16).at[position].set(images)
    )
    send_ids = jnp.full((samp_count * slot_cap,), -1, jnp.int32).at[position].set(slot_ids)
    got_rows, got_ids = (
        lax.all_to_all(
            send_rows.reshape(samp_count, slot_cap, feat_width),
            "samp",
            split_axis=0,
            concat_axis=0,
            tiled=True,
        ),
        lax.all_to_all(
            send_ids.reshape(samp_count, slot_cap), "samp", split_axis=0, concat_axis=0, tiled=True
        ),
    )
    flat_rows = got_rows.reshape(-1, feat_width)
    flat_ids = got_ids.reshape(-1)
    member = jnp.arange(class_cap)[:, None] == flat_ids[None, :]
    class_sums = jnp.dot(member.astype(jnp.bfloat16), flat_rows, preferred_element_type=jnp.float32)
    counts = jnp.sum(member.astype(jnp.float32), axis=1)
    class_means = class_sums / jnp.maximum(counts, 1.0)[:, None]
    col_sums = jnp.sum(images, axis=0, dtype=jnp.float32)
    grand_total = jnp.sum(lax.all_gather(col_sums, "samp"), axis=0)
    center = grand_total / (row_count * samp_count)
    is_valid = flat_ids >= 0
    picked = jnp.take(class_means, jnp.maximum(flat_ids, 0), axis=0)
    centred = jnp.where(is_valid[:, None], flat_rows.astype(jnp.float32) - picked, 0.0).astype(
        jnp.bfloat16
    )
    deviation = (class_means - center[None, :]).astype(jnp.bfloat16)
    part_within = jnp.dot(centred, basis, preferred_element_type=jnp.float32)
    part_between = jnp.dot(deviation, basis, preferred_element_type=jnp.float32)
    full_within, full_between = (
        lax.psum(part_within.astype(jnp.bfloat16), "feat").astype(jnp.float32),
        lax.psum(part_between.astype(jnp.bfloat16), "feat").astype(jnp.float32),
    )
    projected = full_within.astype(jnp.bfloat16)
    weighted = (counts[:, None] * full_between).astype(jnp.bfloat16)
    contract = (((0,), (0,)), ((), ()))
    term_within = lax.dot_general(projected, centred, contract, preferred_element_type=jnp.float32)
    term_between = lax.dot_general(
        weighted, deviation, contract, preferred_element_type=jnp.float32
    )
    k_share = k_width // samp_count
    both = jnp.stack([term_within, term_between]).reshape(2, samp_count, k_share, feat_width)
    swapped = lax.all_to_all(both, "samp", split_axis=1, concat_axis=1, tiled=True)
    summed = jnp.sum(swapped, axis=1)
    within, between = summed[0], summed[1]
    inv_count = 1.0 / (row_count * samp_count)
    return (
        class_means.astype(jnp.bfloat16),
        within.reshape(k_share, feat_width) * inv_count,
        between.reshape(k_share, feat_width) * inv_count,
    )


def solution(mesh):
    in_specs = (P("samp", "feat"), P("samp"), P(), P("feat", None))
    out_specs = (P("samp", "feat"), P("samp", "feat"), P("samp", "feat"))
    return jax.shard_map(
        on_device, mesh=mesh, in_specs=in_specs, out_specs=out_specs, check_vma=False
    )
```

```python
import jax
import jax.numpy as jnp
from jax import lax
from jax.sharding import PartitionSpec as P

CLS_DEV = 192


def on_device(images, labels, owner, basis):
    samp_count = lax.axis_size("samp")
    feat_count = lax.axis_size("feat")
    row_count, feat_width = images.shape
    slot_cap = 2 * row_count // samp_count
    class_cap = CLS_DEV
    class_total = owner.shape[0]
    k_width = basis.shape[1]
    target = jnp.take(owner, labels)
    onehot_dest = (target[:, None] == jnp.arange(samp_count)[None, :]).astype(jnp.int32)
    slot_index = jnp.sum(jnp.cumsum(onehot_dest, axis=0) * onehot_dest, axis=1) - 1
    position = target * slot_cap + slot_index
    same_owner = owner[None, :] == target[:, None]
    earlier = jnp.arange(class_total)[None, :] < labels[:, None]
    slot_ids = jnp.sum((same_owner & earlier).astype(jnp.int32), axis=1)
    send_rows = (
        jnp.zeros((samp_count * slot_cap, feat_width), jnp.bfloat16).at[position].set(images)
    ).reshape(samp_count, slot_cap, feat_width)
    send_ids = jnp.full((samp_count * slot_cap,), -1, jnp.int32).at[position].set(slot_ids)
    id_row = jnp.pad(
        send_ids.reshape(samp_count, slot_cap).astype(jnp.bfloat16),
        ((0, 0), (0, feat_width - slot_cap)),
    )
    col_sums = jnp.sum(images, axis=0, dtype=jnp.float32)
    col_hi = col_sums.astype(jnp.bfloat16)
    col_lo = (col_sums - col_hi.astype(jnp.float32)).astype(jnp.bfloat16)
    extra = jnp.stack([id_row,
                       jnp.broadcast_to(col_hi, (samp_count, feat_width)),
                       jnp.broadcast_to(col_lo, (samp_count, feat_width)),
                       jnp.zeros((samp_count, feat_width), jnp.bfloat16)], axis=1)
    packet = jnp.concatenate([send_rows, extra], axis=1)
    got = lax.all_to_all(packet, "samp", split_axis=0, concat_axis=0, tiled=True)
    flat_rows = got[:, :slot_cap, :].reshape(-1, feat_width)
    flat_ids = got[:, slot_cap, :slot_cap].reshape(-1).astype(jnp.int32)
    grand_total = jnp.sum(
        got[:, slot_cap + 1, :].astype(jnp.float32) + got[:, slot_cap + 2, :].astype(jnp.float32),
        axis=0,
    )
    member = jnp.arange(class_cap)[:, None] == flat_ids[None, :]
    class_sums = jnp.dot(member.astype(jnp.bfloat16), flat_rows, preferred_element_type=jnp.float32)
    counts = jnp.sum(member.astype(jnp.float32), axis=1)
    class_means = class_sums / jnp.maximum(counts, 1.0)[:, None]
    center = grand_total / (row_count * samp_count)
    is_valid = flat_ids >= 0
    picked = jnp.take(class_means, jnp.maximum(flat_ids, 0), axis=0)
    centred = jnp.where(is_valid[:, None], flat_rows.astype(jnp.float32) - picked, 0.0).astype(
        jnp.bfloat16
    )
    deviation = (class_means - center[None, :]).astype(jnp.bfloat16)
    part_within = jnp.dot(centred, basis, preferred_element_type=jnp.float32)
    part_between = jnp.dot(deviation, basis, preferred_element_type=jnp.float32)
    parts = jnp.concatenate([part_within, part_between], axis=0).astype(jnp.bfloat16)
    n_rows = parts.shape[0]
    chunk = n_rows // feat_count
    swapped = lax.all_to_all(
        parts.reshape(feat_count, chunk, k_width), "feat", split_axis=0, concat_axis=0, tiled=True
    )
    reduced = jnp.sum(swapped.astype(jnp.float32), axis=0).astype(jnp.bfloat16)
    spread = lax.all_to_all(
        jnp.broadcast_to(reduced, (feat_count, chunk, k_width)),
        "feat",
        split_axis=0,
        concat_axis=0,
        tiled=True,
    ).reshape(n_rows, k_width)
    n_within = part_within.shape[0]
    projected = spread[:n_within]
    weighted = (counts[:, None] * spread[n_within:].astype(jnp.float32)).astype(jnp.bfloat16)
    contract = (((0,), (0,)), ((), ()))
    term_within = lax.dot_general(projected, centred, contract, preferred_element_type=jnp.float32)
    term_between = lax.dot_general(
        weighted, deviation, contract, preferred_element_type=jnp.float32
    )
    k_share = k_width // samp_count
    both = jnp.stack([term_within, term_between]).reshape(2, samp_count, k_share, feat_width)
    swapped = lax.all_to_all(both, "samp", split_axis=1, concat_axis=1, tiled=True)
    summed = jnp.sum(swapped, axis=1)
    within, between = summed[0], summed[1]
    inv_count = 1.0 / (row_count * samp_count)
    return (class_means.astype(jnp.bfloat16), within * inv_count, between * inv_count)


def solution(mesh):
    in_specs = (P("samp", "feat"), P("samp"), P(), P("feat", None))
    out_specs = (P("samp", "feat"), P("samp", "feat"), P("samp", "feat"))
    return jax.shard_map(
        on_device, mesh=mesh, in_specs=in_specs, out_specs=out_specs, check_vma=False
    )
```

```python
import jax
import jax.numpy as jnp
from jax import lax
from jax.sharding import PartitionSpec as P

CLS_DEV = 192


def on_device(images, labels, owner, basis):
    samp_count = lax.axis_size("samp")
    feat_count = lax.axis_size("feat")
    row_count, feat_width = images.shape
    slot_cap = 2 * row_count // samp_count
    class_cap = CLS_DEV
    class_total = owner.shape[0]
    k_width = basis.shape[1]
    target = jnp.take(owner, labels)
    onehot_dest = (target[:, None] == jnp.arange(samp_count)[None, :]).astype(jnp.int32)
    slot_index = jnp.sum(jnp.cumsum(onehot_dest, axis=0) * onehot_dest, axis=1) - 1
    position = target * slot_cap + slot_index
    same_owner = owner[None, :] == target[:, None]
    earlier = jnp.arange(class_total)[None, :] < labels[:, None]
    slot_ids = jnp.sum((same_owner & earlier).astype(jnp.int32), axis=1)
    send_rows = (
        jnp.zeros((samp_count * slot_cap, feat_width), jnp.bfloat16).at[position].set(images)
    ).reshape(samp_count, slot_cap, feat_width)
    send_ids = jnp.full((samp_count * slot_cap,), -1, jnp.int32).at[position].set(slot_ids)
    id_row = jnp.pad(
        send_ids.reshape(samp_count, slot_cap).astype(jnp.bfloat16),
        ((0, 0), (0, feat_width - slot_cap)),
    )
    col_sums = jnp.sum(images, axis=0, dtype=jnp.float32)
    col_hi = col_sums.astype(jnp.bfloat16)
    col_lo = (col_sums - col_hi.astype(jnp.float32)).astype(jnp.bfloat16)
    extra = jnp.stack([id_row,
                       jnp.broadcast_to(col_hi, (samp_count, feat_width)),
                       jnp.broadcast_to(col_lo, (samp_count, feat_width)),
                       jnp.zeros((samp_count, feat_width), jnp.bfloat16)], axis=1)
    packet = jnp.concatenate([send_rows, extra], axis=1)
    got = lax.all_to_all(packet, "samp", split_axis=0, concat_axis=0, tiled=True)
    flat_rows = got[:, :slot_cap, :].reshape(-1, feat_width)
    flat_ids = got[:, slot_cap, :slot_cap].reshape(-1).astype(jnp.int32)
    grand_total = jnp.sum(
        got[:, slot_cap + 1, :].astype(jnp.float32) + got[:, slot_cap + 2, :].astype(jnp.float32),
        axis=0,
    )
    member = jnp.arange(class_cap)[:, None] == flat_ids[None, :]
    class_sums = jnp.dot(member.astype(jnp.bfloat16), flat_rows, preferred_element_type=jnp.float32)
    counts = jnp.sum(member.astype(jnp.float32), axis=1)
    class_means = class_sums / jnp.maximum(counts, 1.0)[:, None]
    center = grand_total / (row_count * samp_count)
    is_valid = flat_ids >= 0
    picked = jnp.take(class_means, jnp.maximum(flat_ids, 0), axis=0)
    centred = jnp.where(is_valid[:, None], flat_rows.astype(jnp.float32) - picked, 0.0).astype(
        jnp.bfloat16
    )
    deviation = (class_means - center[None, :]).astype(jnp.bfloat16)
    part_within = jnp.dot(centred, basis, preferred_element_type=jnp.float32)
    part_between = jnp.dot(deviation, basis, preferred_element_type=jnp.float32)
    parts = jnp.concatenate([part_within, part_between], axis=0).astype(jnp.bfloat16)
    n_rows = parts.shape[0]
    chunk = n_rows // feat_count
    swapped = lax.all_to_all(
        parts.reshape(feat_count, chunk, k_width), "feat", split_axis=0, concat_axis=0, tiled=True
    )
    reduced = jnp.sum(swapped.astype(jnp.float32), axis=0).astype(jnp.bfloat16)
    spread = lax.all_to_all(
        jnp.broadcast_to(reduced, (feat_count, chunk, k_width)),
        "feat",
        split_axis=0,
        concat_axis=0,
        tiled=True,
    ).reshape(n_rows, k_width)
    n_within = part_within.shape[0]
    projected = spread[:n_within]
    weighted = (counts[:, None] * spread[n_within:].astype(jnp.float32)).astype(jnp.bfloat16)
    contract = (((0,), (0,)), ((), ()))
    term_within = lax.dot_general(projected, centred, contract, preferred_element_type=jnp.float32)
    term_between = lax.dot_general(
        weighted, deviation, contract, preferred_element_type=jnp.float32
    )
    k_share = k_width // samp_count
    both = jnp.stack([term_within, term_between]).reshape(2, samp_count, k_share, feat_width)
    swapped = lax.all_to_all(
        both.astype(jnp.bfloat16), "samp", split_axis=1, concat_axis=1, tiled=True
    )
    summed = jnp.sum(swapped.astype(jnp.float32), axis=1)
    within, between = summed[0], summed[1]
    inv_count = 1.0 / (row_count * samp_count)
    return (class_means.astype(jnp.bfloat16), within * inv_count, between * inv_count)


def solution(mesh):
    in_specs = (P("samp", "feat"), P("samp"), P(), P("feat", None))
    out_specs = (P("samp", "feat"), P("samp", "feat"), P("samp", "feat"))
    return jax.shard_map(
        on_device, mesh=mesh, in_specs=in_specs, out_specs=out_specs, check_vma=False
    )
```

```python
import jax
import jax.numpy as jnp
from jax import lax
from jax.sharding import PartitionSpec as P

CLS_DEV = 192


def on_device(images, labels, owner, basis):
    samp_count = lax.axis_size("samp")
    feat_count = lax.axis_size("feat")
    row_count, feat_width = images.shape
    slot_cap = 2 * row_count // samp_count
    class_cap = CLS_DEV
    class_total = owner.shape[0]
    k_width = basis.shape[1]
    owner_table = (owner[:, None] == jnp.arange(samp_count)[None, :]).astype(jnp.bfloat16)
    class_ids = jnp.arange(class_total)[None, :]
    before = (class_ids < labels[:, None]).astype(jnp.bfloat16)
    is_label = (class_ids == labels[:, None]).astype(jnp.bfloat16)
    tallies = jnp.dot(
        jnp.concatenate([before, is_label], axis=0), owner_table, preferred_element_type=jnp.float32
    )
    below, dest_hot = tallies[:row_count], tallies[row_count:]
    slot_ids = jnp.sum(below * dest_hot, axis=1).astype(jnp.int32)
    onehot_dest = dest_hot.astype(jnp.int32)
    target = jnp.sum(onehot_dest * jnp.arange(samp_count)[None, :], axis=1)
    slot_index = jnp.sum(jnp.cumsum(onehot_dest, axis=0) * onehot_dest, axis=1) - 1
    position = target * slot_cap + slot_index
    place = (jnp.arange(samp_count * slot_cap)[:, None] == position[None, :]).astype(jnp.bfloat16)
    send_rows = (
        jnp.dot(place, images, preferred_element_type=jnp.float32)
        .astype(jnp.bfloat16)
        .reshape(samp_count, slot_cap, feat_width)
    )
    send_ids = (
        jnp.dot(place, (slot_ids + 1).astype(jnp.bfloat16), preferred_element_type=jnp.float32)
        .astype(jnp.int32)
        - 1
    )
    id_row = jnp.pad(
        send_ids.reshape(samp_count, slot_cap).astype(jnp.bfloat16),
        ((0, 0), (0, feat_width - slot_cap)),
    )
    col_sums = jnp.sum(images, axis=0, dtype=jnp.float32)
    col_hi = col_sums.astype(jnp.bfloat16)
    col_lo = (col_sums - col_hi.astype(jnp.float32)).astype(jnp.bfloat16)
    extra = jnp.stack([id_row,
                       jnp.broadcast_to(col_hi, (samp_count, feat_width)),
                       jnp.broadcast_to(col_lo, (samp_count, feat_width)),
                       jnp.zeros((samp_count, feat_width), jnp.bfloat16)], axis=1)
    packet = jnp.concatenate([send_rows, extra], axis=1)
    got = lax.all_to_all(packet, "samp", split_axis=0, concat_axis=0, tiled=True)
    flat_rows = got[:, :slot_cap, :].reshape(-1, feat_width)
    flat_ids = got[:, slot_cap, :slot_cap].reshape(-1).astype(jnp.int32)
    grand_total = jnp.sum(
        got[:, slot_cap + 1, :].astype(jnp.float32) + got[:, slot_cap + 2, :].astype(jnp.float32),
        axis=0,
    )
    member = jnp.arange(class_cap)[:, None] == flat_ids[None, :]
    class_sums = jnp.dot(member.astype(jnp.bfloat16), flat_rows, preferred_element_type=jnp.float32)
    counts = jnp.sum(member.astype(jnp.float32), axis=1)
    class_means = class_sums / jnp.maximum(counts, 1.0)[:, None]
    center = grand_total / (row_count * samp_count)
    is_valid = flat_ids >= 0
    picked = jnp.take(class_means, jnp.maximum(flat_ids, 0), axis=0)
    centred = jnp.where(is_valid[:, None], flat_rows.astype(jnp.float32) - picked, 0.0).astype(
        jnp.bfloat16
    )
    deviation = (class_means - center[None, :]).astype(jnp.bfloat16)
    part_within = jnp.dot(centred, basis, preferred_element_type=jnp.float32)
    part_between = jnp.dot(deviation, basis, preferred_element_type=jnp.float32)
    parts = jnp.concatenate([part_within, part_between], axis=0).astype(jnp.bfloat16)
    n_rows = parts.shape[0]
    chunk = n_rows // feat_count
    swapped = lax.all_to_all(
        parts.reshape(feat_count, chunk, k_width), "feat", split_axis=0, concat_axis=0, tiled=True
    )
    reduced = jnp.sum(swapped.astype(jnp.float32), axis=0).astype(jnp.bfloat16)
    spread = lax.all_to_all(
        jnp.broadcast_to(reduced, (feat_count, chunk, k_width)),
        "feat",
        split_axis=0,
        concat_axis=0,
        tiled=True,
    ).reshape(n_rows, k_width)
    n_within = part_within.shape[0]
    projected = spread[:n_within]
    weighted = (counts[:, None] * spread[n_within:].astype(jnp.float32)).astype(jnp.bfloat16)
    contract = (((0,), (0,)), ((), ()))
    term_within = lax.dot_general(projected, centred, contract, preferred_element_type=jnp.float32)
    term_between = lax.dot_general(
        weighted, deviation, contract, preferred_element_type=jnp.float32
    )
    k_share = k_width // samp_count
    both = jnp.stack([term_within, term_between]).reshape(2, samp_count, k_share, feat_width)
    swapped = lax.all_to_all(
        both.astype(jnp.bfloat16), "samp", split_axis=1, concat_axis=1, tiled=True
    )
    summed = jnp.sum(swapped.astype(jnp.float32), axis=1)
    within, between = summed[0], summed[1]
    inv_count = 1.0 / (row_count * samp_count)
    return (class_means.astype(jnp.bfloat16), within * inv_count, between * inv_count)


def solution(mesh):
    in_specs = (P("samp", "feat"), P("samp"), P(), P("feat", None))
    out_specs = (P("samp", "feat"), P("samp", "feat"), P("samp", "feat"))
    return jax.shard_map(
        on_device, mesh=mesh, in_specs=in_specs, out_specs=out_specs, check_vma=False
    )
```

```python
import jax
import jax.numpy as jnp
from jax import lax
from jax.sharding import PartitionSpec as P

CLS_DEV = 192
SAMP = ("chip", "core")


def on_device(images, labels, owner, basis):
    samp_count = lax.axis_size(SAMP)
    feat_count = lax.axis_size("feat")
    row_count, feat_width = images.shape
    slot_cap = 2 * row_count // samp_count
    class_cap = CLS_DEV
    class_total = owner.shape[0]
    k_width = basis.shape[1]
    owner_table = (owner[:, None] == jnp.arange(samp_count)[None, :]).astype(jnp.bfloat16)
    class_ids = jnp.arange(class_total)[None, :]
    before = (class_ids < labels[:, None]).astype(jnp.bfloat16)
    is_label = (class_ids == labels[:, None]).astype(jnp.bfloat16)
    tallies = jnp.dot(
        jnp.concatenate([before, is_label], axis=0), owner_table, preferred_element_type=jnp.float32
    )
    below, dest_hot = tallies[:row_count], tallies[row_count:]
    slot_ids = jnp.sum(below * dest_hot, axis=1).astype(jnp.int32)
    onehot_dest = dest_hot.astype(jnp.int32)
    target = jnp.sum(onehot_dest * jnp.arange(samp_count)[None, :], axis=1)
    slot_index = jnp.sum(jnp.cumsum(onehot_dest, axis=0) * onehot_dest, axis=1) - 1
    position = target * slot_cap + slot_index
    place = (jnp.arange(samp_count * slot_cap)[:, None] == position[None, :]).astype(jnp.bfloat16)
    send_rows = (
        jnp.dot(place, images, preferred_element_type=jnp.float32)
        .astype(jnp.bfloat16)
        .reshape(samp_count, slot_cap, feat_width)
    )
    send_ids = (
        jnp.dot(place, (slot_ids + 1).astype(jnp.bfloat16), preferred_element_type=jnp.float32)
        .astype(jnp.int32)
        - 1
    )
    id_row = jnp.pad(
        send_ids.reshape(samp_count, slot_cap).astype(jnp.bfloat16),
        ((0, 0), (0, feat_width - slot_cap)),
    )
    col_sums = jnp.sum(images, axis=0, dtype=jnp.float32)
    col_hi = col_sums.astype(jnp.bfloat16)
    col_lo = (col_sums - col_hi.astype(jnp.float32)).astype(jnp.bfloat16)
    extra = jnp.stack([id_row,
                       jnp.broadcast_to(col_hi, (samp_count, feat_width)),
                       jnp.broadcast_to(col_lo, (samp_count, feat_width)),
                       jnp.zeros((samp_count, feat_width), jnp.bfloat16)], axis=1)
    packet = jnp.concatenate([send_rows, extra], axis=1)
    got = lax.all_to_all(packet, SAMP, split_axis=0, concat_axis=0, tiled=True)
    flat_rows = got[:, :slot_cap, :].reshape(-1, feat_width)
    flat_ids = got[:, slot_cap, :slot_cap].reshape(-1).astype(jnp.int32)
    grand_total = jnp.sum(
        got[:, slot_cap + 1, :].astype(jnp.float32) + got[:, slot_cap + 2, :].astype(jnp.float32),
        axis=0,
    )
    member = jnp.arange(class_cap)[:, None] == flat_ids[None, :]
    class_sums = jnp.dot(member.astype(jnp.bfloat16), flat_rows, preferred_element_type=jnp.float32)
    counts = jnp.sum(member.astype(jnp.float32), axis=1)
    class_means = class_sums / jnp.maximum(counts, 1.0)[:, None]
    center = grand_total / (row_count * samp_count)
    is_valid = flat_ids >= 0
    picked = jnp.take(class_means, jnp.maximum(flat_ids, 0), axis=0)
    centred = jnp.where(is_valid[:, None], flat_rows.astype(jnp.float32) - picked, 0.0).astype(
        jnp.bfloat16
    )
    deviation = (class_means - center[None, :]).astype(jnp.bfloat16)
    part_within = jnp.dot(centred, basis, preferred_element_type=jnp.float32)
    part_between = jnp.dot(deviation, basis, preferred_element_type=jnp.float32)
    parts = jnp.concatenate([part_within, part_between], axis=0).astype(jnp.bfloat16)
    n_rows = parts.shape[0]
    chunk = n_rows // feat_count
    swapped = lax.all_to_all(
        parts.reshape(feat_count, chunk, k_width), "feat", split_axis=0, concat_axis=0, tiled=True
    )
    reduced = jnp.sum(swapped.astype(jnp.float32), axis=0).astype(jnp.bfloat16)
    spread = lax.all_to_all(
        jnp.broadcast_to(reduced, (feat_count, chunk, k_width)),
        "feat",
        split_axis=0,
        concat_axis=0,
        tiled=True,
    ).reshape(n_rows, k_width)
    n_within = part_within.shape[0]
    projected = spread[:n_within]
    weighted = (counts[:, None] * spread[n_within:].astype(jnp.float32)).astype(jnp.bfloat16)
    contract = (((0,), (0,)), ((), ()))
    term_within = lax.dot_general(projected, centred, contract, preferred_element_type=jnp.float32)
    term_between = lax.dot_general(
        weighted, deviation, contract, preferred_element_type=jnp.float32
    )
    k_share = k_width // samp_count
    core_count = lax.axis_size("core")
    chip_count = samp_count // core_count
    both = jnp.stack([term_within, term_between]).reshape(
        2, chip_count, core_count, k_share, feat_width
    )
    pair = lax.all_to_all(both, "core", split_axis=2, concat_axis=2, tiled=True)
    per_chip = jnp.sum(pair, axis=2).astype(jnp.bfloat16)
    swapped = lax.all_to_all(per_chip, "chip", split_axis=1, concat_axis=1, tiled=True)
    summed = jnp.sum(swapped.astype(jnp.float32), axis=1)
    within, between = summed[0], summed[1]
    inv_count = 1.0 / (row_count * samp_count)
    return (class_means.astype(jnp.bfloat16), within * inv_count, between * inv_count)


def solution(mesh):
    samp_size = mesh.shape["samp"]
    split = jax.sharding.Mesh(
        mesh.devices.reshape(samp_size // 2, 2, mesh.shape["feat"]), ("chip", "core", "feat")
    )
    in_specs = (P(SAMP, "feat"), P(SAMP), P(), P("feat", None))
    out_specs = (P(SAMP, "feat"), P(SAMP, "feat"), P(SAMP, "feat"))
    return jax.shard_map(
        on_device, mesh=split, in_specs=in_specs, out_specs=out_specs, check_vma=False
    )
```

```python
import jax
import jax.numpy as jnp
from jax import lax
from jax.sharding import PartitionSpec as P

CLS_DEV = 192
SAMP = ("chip", "core")


def on_device(images, labels, owner, basis):
    samp_count = lax.axis_size(SAMP)
    feat_count = lax.axis_size("feat")
    row_count, feat_width = images.shape
    slot_cap = 2 * row_count // samp_count
    class_cap = CLS_DEV
    class_total = owner.shape[0]
    k_width = basis.shape[1]
    owner_table = (owner[:, None] == jnp.arange(samp_count)[None, :]).astype(jnp.bfloat16)
    class_ids = jnp.arange(class_total)[None, :]
    marks = (class_ids < labels[:, None]).astype(jnp.bfloat16) + 256.0 * (
        class_ids == labels[:, None]
    ).astype(jnp.bfloat16)
    tallies = jnp.dot(marks, owner_table, preferred_element_type=jnp.float32)
    dest_hot = (tallies >= 256.0).astype(jnp.float32)
    below = tallies - 256.0 * dest_hot
    slot_ids = jnp.sum(below * dest_hot, axis=1)
    onehot_dest = dest_hot.astype(jnp.int32)
    slot_index = jnp.sum(jnp.cumsum(onehot_dest, axis=0) * onehot_dest, axis=1) - 1
    slot_hot = (slot_index[:, None] == jnp.arange(slot_cap)[None, :]).astype(jnp.float32)
    col_sums = jnp.dot(
        jnp.ones((1, row_count), jnp.bfloat16), images, preferred_element_type=jnp.float32
    )[0]
    col_hi = col_sums.astype(jnp.bfloat16)
    col_lo = (col_sums - col_hi.astype(jnp.float32)).astype(jnp.bfloat16)
    lane = jnp.arange(feat_width)[None, :]
    id_rows = (
        (lane == slot_index[:, None]).astype(jnp.float32) * (slot_ids + 1.0)[:, None]
    ).astype(jnp.bfloat16)
    source = jnp.concatenate(
        [images, id_rows, col_hi[None, :], col_lo[None, :],
         jnp.zeros((6, feat_width), jnp.bfloat16)], axis=0
    )
    to_slot = dest_hot.T[:, None, :] * slot_hot.T[None, :, :]
    pick = jnp.zeros((samp_count, slot_cap + 4, source.shape[0]), jnp.float32)
    pick = pick.at[:, :slot_cap, :row_count].set(to_slot)
    pick = pick.at[:, slot_cap, row_count:2 * row_count].set(dest_hot.T)
    pick = pick.at[:, slot_cap + 1, 2 * row_count].set(1.0)
    pick = pick.at[:, slot_cap + 2, 2 * row_count + 1].set(1.0)
    packet = jnp.einsum(
        "dri,if->drf", pick.astype(jnp.bfloat16), source, preferred_element_type=jnp.float32
    ).astype(jnp.bfloat16)
    got = lax.all_to_all(packet, SAMP, split_axis=0, concat_axis=0, tiled=True)
    flat_rows = got[:, :slot_cap, :].reshape(-1, feat_width)
    flat_ids = got[:, slot_cap, :slot_cap].reshape(-1).astype(jnp.int32) - 1
    grand_total = jnp.sum(
        got[:, slot_cap + 1, :].astype(jnp.float32) + got[:, slot_cap + 2, :].astype(jnp.float32),
        axis=0,
    )
    member = jnp.arange(class_cap)[:, None] == flat_ids[None, :]
    class_sums = jnp.dot(member.astype(jnp.bfloat16), flat_rows, preferred_element_type=jnp.float32)
    counts = jnp.sum(member.astype(jnp.float32), axis=1)
    class_means = class_sums / jnp.maximum(counts, 1.0)[:, None]
    center = grand_total / (row_count * samp_count)
    is_valid = flat_ids >= 0
    picked = jnp.take(class_means, jnp.maximum(flat_ids, 0), axis=0)
    centred = jnp.where(is_valid[:, None], flat_rows.astype(jnp.float32) - picked, 0.0).astype(
        jnp.bfloat16
    )
    deviation = (class_means - center[None, :]).astype(jnp.bfloat16)
    part_within = jnp.dot(centred, basis, preferred_element_type=jnp.float32)
    part_between = jnp.dot(deviation, basis, preferred_element_type=jnp.float32)
    parts = jnp.concatenate([part_within, part_between], axis=0).astype(jnp.bfloat16)
    n_rows = parts.shape[0]
    chunk = n_rows // feat_count
    swapped = lax.all_to_all(
        parts.reshape(feat_count, chunk, k_width), "feat", split_axis=0, concat_axis=0, tiled=True
    )
    reduced = jnp.sum(swapped.astype(jnp.float32), axis=0).astype(jnp.bfloat16)
    spread = lax.all_to_all(
        jnp.broadcast_to(reduced, (feat_count, chunk, k_width)),
        "feat",
        split_axis=0,
        concat_axis=0,
        tiled=True,
    ).reshape(n_rows, k_width)
    n_within = part_within.shape[0]
    projected = spread[:n_within]
    weighted = (counts[:, None] * spread[n_within:].astype(jnp.float32)).astype(jnp.bfloat16)
    contract = (((0,), (0,)), ((), ()))
    term_within = lax.dot_general(projected, centred, contract, preferred_element_type=jnp.float32)
    term_between = lax.dot_general(
        weighted, deviation, contract, preferred_element_type=jnp.float32
    )
    k_share = k_width // samp_count
    core_count = lax.axis_size("core")
    chip_count = samp_count // core_count
    both = jnp.stack([term_within, term_between]).reshape(
        2, chip_count, core_count, k_share, feat_width
    )
    pair = lax.all_to_all(both, "core", split_axis=2, concat_axis=2, tiled=True)
    per_chip = jnp.sum(pair, axis=2).astype(jnp.bfloat16)
    swapped = lax.all_to_all(per_chip, "chip", split_axis=1, concat_axis=1, tiled=True)
    summed = jnp.sum(swapped.astype(jnp.float32), axis=1)
    within, between = summed[0], summed[1]
    inv_count = 1.0 / (row_count * samp_count)
    return (class_means.astype(jnp.bfloat16), within * inv_count, between * inv_count)


def solution(mesh):
    samp_size = mesh.shape["samp"]
    split = jax.sharding.Mesh(
        mesh.devices.reshape(samp_size // 2, 2, mesh.shape["feat"]), ("chip", "core", "feat")
    )
    in_specs = (P(SAMP, "feat"), P(SAMP), P(), P("feat", None))
    out_specs = (P(SAMP, "feat"), P(SAMP, "feat"), P(SAMP, "feat"))
    return jax.shard_map(
        on_device, mesh=split, in_specs=in_specs, out_specs=out_specs, check_vma=False
    )
```

```python
import jax
import jax.numpy as jnp
from jax import lax
from jax.sharding import PartitionSpec as P

CLS_DEV = 192
SAMP = ("chip", "core")


def on_device(images, labels, owner, basis):
    samp_count = lax.axis_size(SAMP)
    feat_count = lax.axis_size("feat")
    row_count, feat_width = images.shape
    slot_cap = 2 * row_count // samp_count
    class_cap = CLS_DEV
    class_total = owner.shape[0]
    k_width = basis.shape[1]
    owner_table = (owner[:, None] == jnp.arange(samp_count)[None, :]).astype(jnp.bfloat16)
    class_ids = jnp.arange(class_total)[None, :]
    marks = (class_ids < labels[:, None]).astype(jnp.bfloat16) + 256.0 * (
        class_ids == labels[:, None]
    ).astype(jnp.bfloat16)
    tallies = jnp.dot(marks, owner_table, preferred_element_type=jnp.float32)
    dest_hot = (tallies >= 256.0).astype(jnp.float32)
    below = tallies - 256.0 * dest_hot
    slot_ids = jnp.sum(below * dest_hot, axis=1)
    onehot_dest = dest_hot.astype(jnp.int32)
    slot_index = jnp.sum(jnp.cumsum(onehot_dest, axis=0) * onehot_dest, axis=1) - 1
    slot_hot = (slot_index[:, None] == jnp.arange(slot_cap)[None, :]).astype(jnp.float32)
    col_sums = jnp.dot(
        jnp.ones((1, row_count), jnp.bfloat16), images, preferred_element_type=jnp.float32
    )[0]
    col_hi = col_sums.astype(jnp.bfloat16)
    col_lo = (col_sums - col_hi.astype(jnp.float32)).astype(jnp.bfloat16)
    lane = jnp.arange(feat_width)[None, :]
    id_rows = (
        (lane == slot_index[:, None]).astype(jnp.float32) * (slot_ids + 1.0)[:, None]
    ).astype(jnp.bfloat16)
    source = jnp.concatenate(
        [images, id_rows, col_hi[None, :], col_lo[None, :],
         jnp.zeros((6, feat_width), jnp.bfloat16)], axis=0
    )
    target = jnp.sum(onehot_dest * jnp.arange(samp_count)[None, :], axis=1)
    tail = source.shape[0] - 2 * row_count
    target_at = jnp.concatenate([target, target, jnp.full((tail,), -1, jnp.int32)])
    slot_at = jnp.concatenate([slot_index, jnp.full((source.shape[0] - row_count,), -1, jnp.int32)])
    d_i = jnp.arange(samp_count)[:, None, None]
    r_i = jnp.arange(slot_cap + 4)[None, :, None]
    s_i = jnp.arange(source.shape[0])[None, None, :]
    to_dest = d_i == target_at[None, None, :]
    pick = (
        (to_dest & (r_i == slot_at[None, None, :]))
        | (to_dest & (r_i == slot_cap) & (s_i >= row_count))
        | ((r_i == slot_cap + 1) & (s_i == 2 * row_count))
        | ((r_i == slot_cap + 2) & (s_i == 2 * row_count + 1))
    )
    packet = jnp.einsum(
        "dri,if->drf", pick.astype(jnp.bfloat16), source, preferred_element_type=jnp.float32
    ).astype(jnp.bfloat16)
    got = lax.all_to_all(packet, SAMP, split_axis=0, concat_axis=0, tiled=True)
    flat_rows = got[:, :slot_cap, :].reshape(-1, feat_width)
    flat_ids = got[:, slot_cap, :slot_cap].reshape(-1).astype(jnp.int32) - 1
    grand_total = jnp.sum(
        got[:, slot_cap + 1, :].astype(jnp.float32) + got[:, slot_cap + 2, :].astype(jnp.float32),
        axis=0,
    )
    member = jnp.arange(class_cap)[:, None] == flat_ids[None, :]
    class_sums = jnp.dot(member.astype(jnp.bfloat16), flat_rows, preferred_element_type=jnp.float32)
    counts = jnp.sum(member.astype(jnp.float32), axis=1)
    class_means = class_sums / jnp.maximum(counts, 1.0)[:, None]
    center = grand_total / (row_count * samp_count)
    is_valid = flat_ids >= 0
    picked = jnp.take(class_means, jnp.maximum(flat_ids, 0), axis=0)
    centred = jnp.where(is_valid[:, None], flat_rows.astype(jnp.float32) - picked, 0.0).astype(
        jnp.bfloat16
    )
    deviation = (class_means - center[None, :]).astype(jnp.bfloat16)
    part_within = jnp.dot(centred, basis, preferred_element_type=jnp.float32)
    part_between = jnp.dot(deviation, basis, preferred_element_type=jnp.float32)
    parts = jnp.concatenate([part_within, part_between], axis=0).astype(jnp.bfloat16)
    n_rows = parts.shape[0]
    chunk = n_rows // feat_count
    swapped = lax.all_to_all(
        parts.reshape(feat_count, chunk, k_width), "feat", split_axis=0, concat_axis=0, tiled=True
    )
    reduced = jnp.sum(swapped.astype(jnp.float32), axis=0).astype(jnp.bfloat16)
    spread = lax.all_to_all(
        jnp.broadcast_to(reduced, (feat_count, chunk, k_width)),
        "feat",
        split_axis=0,
        concat_axis=0,
        tiled=True,
    ).reshape(n_rows, k_width)
    n_within = part_within.shape[0]
    projected = spread[:n_within]
    weighted = (counts[:, None] * spread[n_within:].astype(jnp.float32)).astype(jnp.bfloat16)
    contract = (((0,), (0,)), ((), ()))
    term_within = lax.dot_general(projected, centred, contract, preferred_element_type=jnp.float32)
    term_between = lax.dot_general(
        weighted, deviation, contract, preferred_element_type=jnp.float32
    )
    k_share = k_width // samp_count
    core_count = lax.axis_size("core")
    chip_count = samp_count // core_count
    both = jnp.stack([term_within, term_between]).reshape(
        2, chip_count, core_count, k_share, feat_width
    )
    pair = lax.all_to_all(both, "core", split_axis=2, concat_axis=2, tiled=True)
    per_chip = jnp.sum(pair, axis=2).astype(jnp.bfloat16)
    swapped = lax.all_to_all(per_chip, "chip", split_axis=1, concat_axis=1, tiled=True)
    summed = jnp.sum(swapped.astype(jnp.float32), axis=1)
    within, between = summed[0], summed[1]
    inv_count = 1.0 / (row_count * samp_count)
    return (class_means.astype(jnp.bfloat16), within * inv_count, between * inv_count)


def solution(mesh):
    samp_size = mesh.shape["samp"]
    split = jax.sharding.Mesh(
        mesh.devices.reshape(samp_size // 2, 2, mesh.shape["feat"]), ("chip", "core", "feat")
    )
    in_specs = (P(SAMP, "feat"), P(SAMP), P(), P("feat", None))
    out_specs = (P(SAMP, "feat"), P(SAMP, "feat"), P(SAMP, "feat"))
    return jax.shard_map(
        on_device, mesh=split, in_specs=in_specs, out_specs=out_specs, check_vma=False
    )
```

```python
import jax
import jax.numpy as jnp
from jax import lax
from jax.sharding import PartitionSpec as P

CLS_DEV = 192
SAMP = ("chip", "core")


def on_device(images, labels, owner, basis):
    samp_count = lax.axis_size(SAMP)
    feat_count = lax.axis_size("feat")
    row_count, feat_width = images.shape
    slot_cap = 2 * row_count // samp_count
    class_cap = CLS_DEV
    class_total = owner.shape[0]
    k_width = basis.shape[1]
    owner_table = (owner[:, None] == jnp.arange(samp_count)[None, :]).astype(jnp.bfloat16)
    class_ids = jnp.arange(class_total)[None, :]
    marks = (class_ids < labels[:, None]).astype(jnp.bfloat16) + 256.0 * (
        class_ids == labels[:, None]
    ).astype(jnp.bfloat16)
    tallies = jnp.dot(marks, owner_table, preferred_element_type=jnp.float32)
    dest_hot = (tallies >= 256.0).astype(jnp.float32)
    below = tallies - 256.0 * dest_hot
    slot_ids = jnp.sum(below * dest_hot, axis=1)
    onehot_dest = dest_hot.astype(jnp.int32)
    slot_index = jnp.sum(jnp.cumsum(onehot_dest, axis=0) * onehot_dest, axis=1) - 1
    slot_hot = (slot_index[:, None] == jnp.arange(slot_cap)[None, :]).astype(jnp.float32)
    col_sums = jnp.dot(
        jnp.ones((1, row_count), jnp.bfloat16), images, preferred_element_type=jnp.float32
    )[0]
    col_hi = col_sums.astype(jnp.bfloat16)
    col_lo = (col_sums - col_hi.astype(jnp.float32)).astype(jnp.bfloat16)
    lane = jnp.arange(feat_width)[None, :]
    id_rows = (
        (lane == slot_index[:, None]).astype(jnp.float32) * (slot_ids + 1.0)[:, None]
    ).astype(jnp.bfloat16)
    source = jnp.concatenate(
        [images, id_rows, col_hi[None, :], col_lo[None, :],
         jnp.zeros((6, feat_width), jnp.bfloat16)], axis=0
    )
    target = jnp.sum(onehot_dest * jnp.arange(samp_count)[None, :], axis=1)
    tail = source.shape[0] - 2 * row_count
    target_at = jnp.concatenate([target, target, jnp.full((tail,), -1, jnp.int32)])
    slot_at = jnp.concatenate([slot_index, jnp.full((source.shape[0] - row_count,), -1, jnp.int32)])
    d_i = jnp.arange(samp_count)[:, None, None]
    r_i = jnp.arange(slot_cap + 4)[None, :, None]
    s_i = jnp.arange(source.shape[0])[None, None, :]
    to_dest = d_i == target_at[None, None, :]
    pick = (
        (to_dest & (r_i == slot_at[None, None, :]))
        | (to_dest & (r_i == slot_cap) & (s_i >= row_count))
        | ((r_i == slot_cap + 1) & (s_i == 2 * row_count))
        | ((r_i == slot_cap + 2) & (s_i == 2 * row_count + 1))
    )
    packet = jnp.einsum(
        "dri,if->drf", pick.astype(jnp.bfloat16), source, preferred_element_type=jnp.float32
    ).astype(jnp.bfloat16)
    got = lax.all_to_all(packet, SAMP, split_axis=0, concat_axis=0, tiled=True)
    flat_rows = got[:, :slot_cap, :].reshape(-1, feat_width)
    flat_ids = got[:, slot_cap, :slot_cap].reshape(-1).astype(jnp.int32) - 1
    grand_total = jnp.sum(
        got[:, slot_cap + 1, :].astype(jnp.float32) + got[:, slot_cap + 2, :].astype(jnp.float32),
        axis=0,
    )
    member = jnp.arange(class_cap)[:, None] == flat_ids[None, :]
    class_sums = jnp.dot(member.astype(jnp.bfloat16), flat_rows, preferred_element_type=jnp.float32)
    counts = jnp.sum(member.astype(jnp.float32), axis=1)
    class_means = class_sums / jnp.maximum(counts, 1.0)[:, None]
    center = grand_total / (row_count * samp_count)
    is_valid = flat_ids >= 0
    mean_hi = class_means.astype(jnp.bfloat16)
    rest = class_means - mean_hi.astype(jnp.float32)
    mean_mid = rest.astype(jnp.bfloat16)
    mean_lo = (rest - mean_mid.astype(jnp.float32)).astype(jnp.bfloat16)
    lookup = member.T.astype(jnp.bfloat16)
    picked = (
        jnp.dot(lookup, mean_hi, preferred_element_type=jnp.float32)
        + jnp.dot(lookup, mean_mid, preferred_element_type=jnp.float32)
    ) + jnp.dot(lookup, mean_lo, preferred_element_type=jnp.float32)
    centred = jnp.where(is_valid[:, None], flat_rows.astype(jnp.float32) - picked, 0.0).astype(
        jnp.bfloat16
    )
    deviation = (class_means - center[None, :]).astype(jnp.bfloat16)
    part_within = jnp.dot(centred, basis, preferred_element_type=jnp.float32)
    part_between = jnp.dot(deviation, basis, preferred_element_type=jnp.float32)
    parts = jnp.concatenate([part_within, part_between], axis=0).astype(jnp.bfloat16)
    n_rows = parts.shape[0]
    chunk = n_rows // feat_count
    swapped = lax.all_to_all(
        parts.reshape(feat_count, chunk, k_width), "feat", split_axis=0, concat_axis=0, tiled=True
    )
    copies = jnp.einsum(
        "jcn,jd->dcn", swapped, jnp.ones((feat_count, feat_count), jnp.bfloat16),
        preferred_element_type=jnp.float32,
    ).astype(jnp.bfloat16)
    spread = lax.all_to_all(
        copies,
        "feat",
        split_axis=0,
        concat_axis=0,
        tiled=True,
    ).reshape(n_rows, k_width)
    n_within = part_within.shape[0]
    projected = spread[:n_within]
    weighted = (counts[:, None] * spread[n_within:].astype(jnp.float32)).astype(jnp.bfloat16)
    contract = (((0,), (0,)), ((), ()))
    term_within = lax.dot_general(projected, centred, contract, preferred_element_type=jnp.float32)
    term_between = lax.dot_general(
        weighted, deviation, contract, preferred_element_type=jnp.float32
    )
    k_share = k_width // samp_count
    core_count = lax.axis_size("core")
    chip_count = samp_count // core_count
    both = jnp.stack([term_within, term_between]).reshape(
        2, chip_count, core_count, k_share, feat_width
    )
    pair = lax.all_to_all(both, "core", split_axis=2, concat_axis=2, tiled=True)
    per_chip = jnp.sum(pair, axis=2).astype(jnp.bfloat16)
    swapped = lax.all_to_all(per_chip, "chip", split_axis=1, concat_axis=1, tiled=True)
    summed = jnp.sum(swapped.astype(jnp.float32), axis=1)
    within, between = summed[0], summed[1]
    inv_count = 1.0 / (row_count * samp_count)
    return (class_means.astype(jnp.bfloat16), within * inv_count, between * inv_count)


def solution(mesh):
    samp_size = mesh.shape["samp"]
    split = jax.sharding.Mesh(
        mesh.devices.reshape(samp_size // 2, 2, mesh.shape["feat"]), ("chip", "core", "feat")
    )
    in_specs = (P(SAMP, "feat"), P(SAMP), P(), P("feat", None))
    out_specs = (P(SAMP, "feat"), P(SAMP, "feat"), P(SAMP, "feat"))
    return jax.shard_map(
        on_device, mesh=split, in_specs=in_specs, out_specs=out_specs, check_vma=False
    )
```

```python
import jax
import jax.numpy as jnp
from jax import lax
from jax.sharding import PartitionSpec as P

CLS_DEV = 192
SAMP = ("chip", "core")


def on_device(images, labels, owner, basis):
    samp_count = lax.axis_size(SAMP)
    feat_count = lax.axis_size("feat")
    row_count, feat_width = images.shape
    slot_cap = 2 * row_count // samp_count
    class_cap = CLS_DEV
    class_total = owner.shape[0]
    k_width = basis.shape[1]
    owner_table = (owner[:, None] == jnp.arange(samp_count)[None, :]).astype(jnp.bfloat16)
    class_ids = jnp.arange(class_total)[None, :]
    marks = (class_ids < labels[:, None]).astype(jnp.bfloat16) + 256.0 * (
        class_ids == labels[:, None]
    ).astype(jnp.bfloat16)
    tallies = jnp.dot(marks, owner_table, preferred_element_type=jnp.float32)
    dest_hot = (tallies >= 256.0).astype(jnp.float32)
    below = tallies - 256.0 * dest_hot
    slot_ids = jnp.sum(below * dest_hot, axis=1)
    onehot_dest = dest_hot.astype(jnp.int32)
    slot_index = jnp.sum(jnp.cumsum(onehot_dest, axis=0) * onehot_dest, axis=1) - 1
    slot_hot = (slot_index[:, None] == jnp.arange(slot_cap)[None, :]).astype(jnp.float32)
    col_sums = jnp.dot(
        jnp.ones((1, row_count), jnp.bfloat16), images, preferred_element_type=jnp.float32
    )[0]
    col_hi = col_sums.astype(jnp.bfloat16)
    col_lo = (col_sums - col_hi.astype(jnp.float32)).astype(jnp.bfloat16)
    lane = jnp.arange(feat_width)[None, :]
    id_rows = (
        (lane == slot_index[:, None]).astype(jnp.float32) * (slot_ids + 1.0)[:, None]
    ).astype(jnp.bfloat16)
    source = jnp.concatenate(
        [images, id_rows, col_hi[None, :], col_lo[None, :],
         jnp.zeros((6, feat_width), jnp.bfloat16)], axis=0
    )
    target = jnp.sum(onehot_dest * jnp.arange(samp_count)[None, :], axis=1)
    tail = source.shape[0] - 2 * row_count
    target_at = jnp.concatenate([target, target, jnp.full((tail,), -1, jnp.int32)])
    slot_at = jnp.concatenate([slot_index, jnp.full((source.shape[0] - row_count,), -1, jnp.int32)])
    d_i = jnp.arange(samp_count)[:, None, None]
    r_i = jnp.arange(slot_cap + 4)[None, :, None]
    s_i = jnp.arange(source.shape[0])[None, None, :]
    to_dest = d_i == target_at[None, None, :]
    pick = (
        (to_dest & (r_i == slot_at[None, None, :]))
        | (to_dest & (r_i == slot_cap) & (s_i >= row_count))
        | ((r_i == slot_cap + 1) & (s_i == 2 * row_count))
        | ((r_i == slot_cap + 2) & (s_i == 2 * row_count + 1))
    )
    packet = jnp.einsum(
        "dri,if->drf", pick.astype(jnp.bfloat16), source, preferred_element_type=jnp.float32
    ).astype(jnp.bfloat16)
    got = lax.all_to_all(packet, SAMP, split_axis=0, concat_axis=0, tiled=True)
    flat_rows = got[:, :slot_cap, :].reshape(-1, feat_width)
    flat_ids = got[:, slot_cap, :slot_cap].reshape(-1).astype(jnp.int32) - 1
    grand_total = jnp.sum(
        got[:, slot_cap + 1, :].astype(jnp.float32) + got[:, slot_cap + 2, :].astype(jnp.float32),
        axis=0,
    )
    member = jnp.arange(class_cap)[:, None] == flat_ids[None, :]
    class_sums = jnp.dot(member.astype(jnp.bfloat16), flat_rows, preferred_element_type=jnp.float32)
    counts = jnp.sum(member.astype(jnp.float32), axis=1)
    class_means = class_sums / jnp.maximum(counts, 1.0)[:, None]
    center = grand_total / (row_count * samp_count)
    is_valid = flat_ids >= 0
    hi_part = lax.reduce_precision(class_means, exponent_bits=8, mantissa_bits=7)
    rest = class_means - hi_part
    mid_part = lax.reduce_precision(rest, exponent_bits=8, mantissa_bits=7)
    mean_hi = hi_part.astype(jnp.bfloat16)
    mean_mid = mid_part.astype(jnp.bfloat16)
    mean_lo = (rest - mid_part).astype(jnp.bfloat16)
    lookup = member.T.astype(jnp.bfloat16)
    picked = (
        jnp.dot(lookup, mean_hi, preferred_element_type=jnp.float32)
        + jnp.dot(lookup, mean_mid, preferred_element_type=jnp.float32)
    ) + jnp.dot(lookup, mean_lo, preferred_element_type=jnp.float32)
    centred = jnp.where(is_valid[:, None], flat_rows.astype(jnp.float32) - picked, 0.0).astype(
        jnp.bfloat16
    )
    deviation = (class_means - center[None, :]).astype(jnp.bfloat16)
    part_within = jnp.dot(centred, basis, preferred_element_type=jnp.float32)
    part_between = jnp.dot(deviation, basis, preferred_element_type=jnp.float32)
    parts = jnp.concatenate([part_within, part_between], axis=0).astype(jnp.bfloat16)
    n_rows = parts.shape[0]
    chunk = n_rows // feat_count
    swapped = lax.all_to_all(
        parts.reshape(feat_count, chunk, k_width), "feat", split_axis=0, concat_axis=0, tiled=True
    )
    copies = jnp.einsum(
        "jcn,jd->dcn", swapped, jnp.ones((feat_count, feat_count), jnp.bfloat16),
        preferred_element_type=jnp.float32,
    ).astype(jnp.bfloat16)
    spread = lax.all_to_all(
        copies,
        "feat",
        split_axis=0,
        concat_axis=0,
        tiled=True,
    ).reshape(n_rows, k_width)
    n_within = part_within.shape[0]
    projected = spread[:n_within]
    weighted = (counts[:, None] * spread[n_within:].astype(jnp.float32)).astype(jnp.bfloat16)
    contract = (((0,), (0,)), ((), ()))
    term_within = lax.dot_general(projected, centred, contract, preferred_element_type=jnp.float32)
    term_between = lax.dot_general(
        weighted, deviation, contract, preferred_element_type=jnp.float32
    )
    k_share = k_width // samp_count
    core_count = lax.axis_size("core")
    chip_count = samp_count // core_count
    both = jnp.stack([term_within, term_between]).reshape(
        2, chip_count, core_count, k_share, feat_width
    )
    pair = lax.all_to_all(both, "core", split_axis=2, concat_axis=2, tiled=True)
    per_chip = jnp.sum(pair, axis=2).astype(jnp.bfloat16)
    swapped = lax.all_to_all(per_chip, "chip", split_axis=1, concat_axis=1, tiled=True)
    summed = jnp.sum(swapped.astype(jnp.float32), axis=1)
    within, between = summed[0], summed[1]
    inv_count = 1.0 / (row_count * samp_count)
    return (class_means.astype(jnp.bfloat16), within * inv_count, between * inv_count)


def solution(mesh):
    samp_size = mesh.shape["samp"]
    split = jax.sharding.Mesh(
        mesh.devices.reshape(samp_size // 2, 2, mesh.shape["feat"]), ("chip", "core", "feat")
    )
    in_specs = (P(SAMP, "feat"), P(SAMP), P(), P("feat", None))
    out_specs = (P(SAMP, "feat"), P(SAMP, "feat"), P(SAMP, "feat"))
    return jax.shard_map(
        on_device, mesh=split, in_specs=in_specs, out_specs=out_specs, check_vma=False
    )
```

```python
import jax
import jax.numpy as jnp
from jax import lax
from jax.sharding import PartitionSpec as P

CLS_DEV = 192
SAMP = ("chip", "core")


def on_device(images, labels, owner, basis):
    samp_count = lax.axis_size(SAMP)
    feat_count = lax.axis_size("feat")
    row_count, feat_width = images.shape
    slot_cap = 2 * row_count // samp_count
    class_cap = CLS_DEV
    class_total = owner.shape[0]
    k_width = basis.shape[1]
    owner_table = (owner[:, None] == jnp.arange(samp_count)[None, :]).astype(jnp.bfloat16)
    class_ids = jnp.arange(class_total)[None, :]
    marks = (class_ids < labels[:, None]).astype(jnp.bfloat16) + 256.0 * (
        class_ids == labels[:, None]
    ).astype(jnp.bfloat16)
    tallies = jnp.dot(marks, owner_table, preferred_element_type=jnp.float32)
    dest_hot = (tallies >= 256.0).astype(jnp.float32)
    below = tallies - 256.0 * dest_hot
    slot_ids = jnp.sum(below * dest_hot, axis=1)
    onehot_dest = dest_hot.astype(jnp.int32)
    slot_index = jnp.sum(jnp.cumsum(onehot_dest, axis=0) * onehot_dest, axis=1) - 1
    slot_hot = (slot_index[:, None] == jnp.arange(slot_cap)[None, :]).astype(jnp.float32)
    lane = jnp.arange(feat_width)[None, :]
    id_rows = (
        (lane == slot_index[:, None]).astype(jnp.float32) * (slot_ids + 1.0)[:, None]
    ).astype(jnp.bfloat16)
    source = jnp.concatenate([images, id_rows], axis=0)
    target = jnp.sum(onehot_dest * jnp.arange(samp_count)[None, :], axis=1)
    tail = source.shape[0] - 2 * row_count
    target_at = jnp.concatenate([target, target, jnp.full((tail,), -1, jnp.int32)])
    slot_at = jnp.concatenate([slot_index, jnp.full((source.shape[0] - row_count,), -1, jnp.int32)])
    d_i = jnp.arange(samp_count)[:, None, None]
    r_i = jnp.arange(slot_cap + 4)[None, :, None]
    s_i = jnp.arange(source.shape[0])[None, None, :]
    to_dest = d_i == target_at[None, None, :]
    pick = (
        (to_dest & (r_i == slot_at[None, None, :]))
        | (to_dest & (r_i == slot_cap) & (s_i >= row_count))
        | ((r_i == slot_cap + 1) & (s_i < row_count))
    )
    wide = jnp.einsum(
        "dri,if->drf", pick.astype(jnp.bfloat16), source, preferred_element_type=jnp.float32
    )
    col_sums = wide[:, slot_cap + 1, :]
    col_lo = col_sums - lax.reduce_precision(col_sums, exponent_bits=8, mantissa_bits=7)
    packet = jnp.where(r_i[0] == slot_cap + 2, col_lo[:, None, :], wide).astype(jnp.bfloat16)
    got = lax.all_to_all(packet, SAMP, split_axis=0, concat_axis=0, tiled=True)
    flat_rows = got[:, :slot_cap, :].reshape(-1, feat_width)
    flat_ids = got[:, slot_cap, :slot_cap].reshape(-1).astype(jnp.int32) - 1
    grand_total = jnp.sum(
        got[:, slot_cap + 1, :].astype(jnp.float32) + got[:, slot_cap + 2, :].astype(jnp.float32),
        axis=0,
    )
    member = jnp.arange(class_cap)[:, None] == flat_ids[None, :]
    class_sums = jnp.dot(member.astype(jnp.bfloat16), flat_rows, preferred_element_type=jnp.float32)
    counts = jnp.sum(member.astype(jnp.float32), axis=1)
    class_means = class_sums / jnp.maximum(counts, 1.0)[:, None]
    center = grand_total / (row_count * samp_count)
    is_valid = flat_ids >= 0
    hi_part = lax.reduce_precision(class_means, exponent_bits=8, mantissa_bits=7)
    rest = class_means - hi_part
    mid_part = lax.reduce_precision(rest, exponent_bits=8, mantissa_bits=7)
    mean_hi = hi_part.astype(jnp.bfloat16)
    mean_mid = mid_part.astype(jnp.bfloat16)
    mean_lo = (rest - mid_part).astype(jnp.bfloat16)
    lookup = member.T.astype(jnp.bfloat16)
    picked = (
        jnp.dot(lookup, mean_hi, preferred_element_type=jnp.float32)
        + jnp.dot(lookup, mean_mid, preferred_element_type=jnp.float32)
    ) + jnp.dot(lookup, mean_lo, preferred_element_type=jnp.float32)
    centred = jnp.where(is_valid[:, None], flat_rows.astype(jnp.float32) - picked, 0.0).astype(
        jnp.bfloat16
    )
    deviation = (class_means - center[None, :]).astype(jnp.bfloat16)
    part_within = jnp.dot(centred, basis, preferred_element_type=jnp.float32)
    part_between = jnp.dot(deviation, basis, preferred_element_type=jnp.float32)
    parts = jnp.concatenate([part_within, part_between], axis=0).astype(jnp.bfloat16)
    n_rows = parts.shape[0]
    chunk = n_rows // feat_count
    swapped = lax.all_to_all(
        parts.reshape(feat_count, chunk, k_width), "feat", split_axis=0, concat_axis=0, tiled=True
    )
    copies = jnp.einsum(
        "jcn,jd->dcn", swapped, jnp.ones((feat_count, feat_count), jnp.bfloat16),
        preferred_element_type=jnp.float32,
    ).astype(jnp.bfloat16)
    spread = lax.all_to_all(
        copies,
        "feat",
        split_axis=0,
        concat_axis=0,
        tiled=True,
    ).reshape(n_rows, k_width)
    n_within = part_within.shape[0]
    projected = spread[:n_within]
    weighted = (counts[:, None] * spread[n_within:].astype(jnp.float32)).astype(jnp.bfloat16)
    contract = (((0,), (0,)), ((), ()))
    term_within = lax.dot_general(projected, centred, contract, preferred_element_type=jnp.float32)
    term_between = lax.dot_general(
        weighted, deviation, contract, preferred_element_type=jnp.float32
    )
    k_share = k_width // samp_count
    core_count = lax.axis_size("core")
    chip_count = samp_count // core_count
    both = jnp.stack([term_within, term_between]).reshape(
        2, chip_count, core_count, k_share, feat_width
    )
    pair = lax.all_to_all(both, "core", split_axis=2, concat_axis=2, tiled=True)
    per_chip = jnp.sum(pair, axis=2).astype(jnp.bfloat16)
    swapped = lax.all_to_all(per_chip, "chip", split_axis=1, concat_axis=1, tiled=True)
    summed = jnp.sum(swapped.astype(jnp.float32), axis=1)
    within, between = summed[0], summed[1]
    inv_count = 1.0 / (row_count * samp_count)
    return (class_means.astype(jnp.bfloat16), within * inv_count, between * inv_count)


def solution(mesh):
    samp_size = mesh.shape["samp"]
    split = jax.sharding.Mesh(
        mesh.devices.reshape(samp_size // 2, 2, mesh.shape["feat"]), ("chip", "core", "feat")
    )
    in_specs = (P(SAMP, "feat"), P(SAMP), P(), P("feat", None))
    out_specs = (P(SAMP, "feat"), P(SAMP, "feat"), P(SAMP, "feat"))
    return jax.shard_map(
        on_device, mesh=split, in_specs=in_specs, out_specs=out_specs, check_vma=False
    )
```

```python
import jax
import jax.numpy as jnp
from jax import lax
from jax.sharding import PartitionSpec as P

CLS_DEV = 192
SAMP = ("chip", "core")


def on_device(images, labels, owner, basis):
    samp_count = lax.axis_size(SAMP)
    feat_count = lax.axis_size("feat")
    row_count, feat_width = images.shape
    slot_cap = 2 * row_count // samp_count
    class_cap = CLS_DEV
    class_total = owner.shape[0]
    k_width = basis.shape[1]
    owner_table = (owner[:, None] == jnp.arange(samp_count)[None, :]).astype(jnp.bfloat16)
    blk = 64
    n_blocks = class_total // blk
    block_of = labels // blk
    within_blk = labels % blk
    owner_blocks = owner_table.reshape(n_blocks, blk * samp_count)
    block_counts = jnp.sum(
        owner_table.reshape(n_blocks, blk, samp_count).astype(jnp.float32), axis=1
    ).astype(jnp.bfloat16)
    earlier_blocks = (
        jnp.arange(n_blocks)[None, :] < jnp.arange(n_blocks)[:, None]
    ).astype(jnp.bfloat16)
    prefix = jnp.dot(earlier_blocks, block_counts, preferred_element_type=jnp.float32)
    block_hot = (block_of[:, None] == jnp.arange(n_blocks)[None, :]).astype(jnp.bfloat16)
    base = jnp.dot(block_hot, prefix.astype(jnp.bfloat16), preferred_element_type=jnp.float32)
    rows_of = jnp.dot(block_hot, owner_blocks, preferred_element_type=jnp.float32).reshape(
        row_count, blk, samp_count
    )
    spot = jnp.arange(blk)[None, :, None]
    below = base + jnp.sum(jnp.where(spot < within_blk[:, None, None], rows_of, 0.0), axis=1)
    dest_hot = jnp.sum(jnp.where(spot == within_blk[:, None, None], rows_of, 0.0), axis=1)
    slot_ids = jnp.sum(below * dest_hot, axis=1)
    onehot_dest = dest_hot.astype(jnp.int32)
    slot_index = jnp.sum(jnp.cumsum(onehot_dest, axis=0) * onehot_dest, axis=1) - 1
    slot_hot = (slot_index[:, None] == jnp.arange(slot_cap)[None, :]).astype(jnp.float32)
    lane = jnp.arange(feat_width)[None, :]
    id_rows = (
        (lane == slot_index[:, None]).astype(jnp.float32) * (slot_ids + 1.0)[:, None]
    ).astype(jnp.bfloat16)
    source = jnp.concatenate([images, id_rows], axis=0)
    target = jnp.sum(onehot_dest * jnp.arange(samp_count)[None, :], axis=1)
    tail = source.shape[0] - 2 * row_count
    target_at = jnp.concatenate([target, target, jnp.full((tail,), -1, jnp.int32)])
    slot_at = jnp.concatenate([slot_index, jnp.full((source.shape[0] - row_count,), -1, jnp.int32)])
    d_i = jnp.arange(samp_count)[:, None, None]
    r_i = jnp.arange(slot_cap + 4)[None, :, None]
    s_i = jnp.arange(source.shape[0])[None, None, :]
    to_dest = d_i == target_at[None, None, :]
    pick = (
        (to_dest & (r_i == slot_at[None, None, :]))
        | (to_dest & (r_i == slot_cap) & (s_i >= row_count))
        | ((r_i == slot_cap + 1) & (s_i < row_count))
    )
    wide = jnp.einsum(
        "dri,if->drf", pick.astype(jnp.bfloat16), source, preferred_element_type=jnp.float32
    )
    col_sums = wide[:, slot_cap + 1, :]
    col_lo = col_sums - lax.reduce_precision(col_sums, exponent_bits=8, mantissa_bits=7)
    packet = jnp.where(r_i[0] == slot_cap + 2, col_lo[:, None, :], wide).astype(jnp.bfloat16)
    got = lax.all_to_all(packet, SAMP, split_axis=0, concat_axis=0, tiled=True)
    flat_rows = got[:, :slot_cap, :].reshape(-1, feat_width)
    flat_ids = got[:, slot_cap, :slot_cap].reshape(-1).astype(jnp.int32) - 1
    grand_total = jnp.sum(
        got[:, slot_cap + 1, :].astype(jnp.float32) + got[:, slot_cap + 2, :].astype(jnp.float32),
        axis=0,
    )
    member = jnp.arange(class_cap)[:, None] == flat_ids[None, :]
    class_sums = jnp.dot(member.astype(jnp.bfloat16), flat_rows, preferred_element_type=jnp.float32)
    counts = jnp.sum(member.astype(jnp.float32), axis=1)
    class_means = class_sums / jnp.maximum(counts, 1.0)[:, None]
    center = grand_total / (row_count * samp_count)
    is_valid = flat_ids >= 0
    hi_part = lax.reduce_precision(class_means, exponent_bits=8, mantissa_bits=7)
    rest = class_means - hi_part
    mid_part = lax.reduce_precision(rest, exponent_bits=8, mantissa_bits=7)
    mean_hi = hi_part.astype(jnp.bfloat16)
    mean_mid = mid_part.astype(jnp.bfloat16)
    mean_lo = (rest - mid_part).astype(jnp.bfloat16)
    lookup = member.T.astype(jnp.bfloat16)
    picked = (
        jnp.dot(lookup, mean_hi, preferred_element_type=jnp.float32)
        + jnp.dot(lookup, mean_mid, preferred_element_type=jnp.float32)
    ) + jnp.dot(lookup, mean_lo, preferred_element_type=jnp.float32)
    centred = jnp.where(is_valid[:, None], flat_rows.astype(jnp.float32) - picked, 0.0).astype(
        jnp.bfloat16
    )
    deviation = (class_means - center[None, :]).astype(jnp.bfloat16)
    part_within = jnp.dot(centred, basis, preferred_element_type=jnp.float32)
    part_between = jnp.dot(deviation, basis, preferred_element_type=jnp.float32)
    parts = jnp.concatenate([part_within, part_between], axis=0).astype(jnp.bfloat16)
    n_rows = parts.shape[0]
    chunk = n_rows // feat_count
    swapped = lax.all_to_all(
        parts.reshape(feat_count, chunk, k_width), "feat", split_axis=0, concat_axis=0, tiled=True
    )
    copies = jnp.einsum(
        "jcn,jd->dcn", swapped, jnp.ones((feat_count, feat_count), jnp.bfloat16),
        preferred_element_type=jnp.float32,
    ).astype(jnp.bfloat16)
    spread = lax.all_to_all(
        copies,
        "feat",
        split_axis=0,
        concat_axis=0,
        tiled=True,
    ).reshape(n_rows, k_width)
    n_within = part_within.shape[0]
    projected = spread[:n_within]
    weighted = (counts[:, None] * spread[n_within:].astype(jnp.float32)).astype(jnp.bfloat16)
    contract = (((0,), (0,)), ((), ()))
    term_within = lax.dot_general(projected, centred, contract, preferred_element_type=jnp.float32)
    term_between = lax.dot_general(
        weighted, deviation, contract, preferred_element_type=jnp.float32
    )
    k_share = k_width // samp_count
    core_count = lax.axis_size("core")
    chip_count = samp_count // core_count
    both = jnp.stack([term_within, term_between]).reshape(
        2, chip_count, core_count, k_share, feat_width
    )
    pair = lax.all_to_all(both, "core", split_axis=2, concat_axis=2, tiled=True)
    per_chip = jnp.sum(pair, axis=2).astype(jnp.bfloat16)
    swapped = lax.all_to_all(per_chip, "chip", split_axis=1, concat_axis=1, tiled=True)
    summed = jnp.sum(swapped.astype(jnp.float32), axis=1)
    within, between = summed[0], summed[1]
    inv_count = 1.0 / (row_count * samp_count)
    return (class_means.astype(jnp.bfloat16), within * inv_count, between * inv_count)


def solution(mesh):
    samp_size = mesh.shape["samp"]
    split = jax.sharding.Mesh(
        mesh.devices.reshape(samp_size // 2, 2, mesh.shape["feat"]), ("chip", "core", "feat")
    )
    in_specs = (P(SAMP, "feat"), P(SAMP), P(), P("feat", None))
    out_specs = (P(SAMP, "feat"), P(SAMP, "feat"), P(SAMP, "feat"))
    return jax.shard_map(
        on_device, mesh=split, in_specs=in_specs, out_specs=out_specs, check_vma=False
    )
```

```python
import jax
import jax.numpy as jnp
from jax import lax
from jax.sharding import PartitionSpec as P

CLS_DEV = 192
SAMP = ("chip", "core")


def on_device(images, labels, owner, basis):
    samp_count = lax.axis_size(SAMP)
    feat_count = lax.axis_size("feat")
    row_count, feat_width = images.shape
    slot_cap = 2 * row_count // samp_count
    class_cap = CLS_DEV
    class_total = owner.shape[0]
    k_width = basis.shape[1]
    owner_table = (owner[:, None] == jnp.arange(samp_count)[None, :]).astype(jnp.bfloat16)
    class_ids = jnp.arange(class_total)[None, :]
    marks = (class_ids < labels[:, None]).astype(jnp.bfloat16) + 256.0 * (
        class_ids == labels[:, None]
    ).astype(jnp.bfloat16)
    tallies = jnp.dot(marks, owner_table, preferred_element_type=jnp.float32)
    dest_hot = (tallies >= 256.0).astype(jnp.float32)
    below = tallies - 256.0 * dest_hot
    slot_ids = jnp.sum(below * dest_hot, axis=1)
    onehot_dest = dest_hot.astype(jnp.int32)
    slot_index = jnp.sum(jnp.cumsum(onehot_dest, axis=0) * onehot_dest, axis=1) - 1
    slot_hot = (slot_index[:, None] == jnp.arange(slot_cap)[None, :]).astype(jnp.float32)
    lane = jnp.arange(feat_width)[None, :]
    id_rows = (
        (lane == slot_index[:, None]).astype(jnp.float32) * (slot_ids + 1.0)[:, None]
    ).astype(jnp.bfloat16)
    source = jnp.concatenate([images, id_rows], axis=0)
    target = jnp.sum(onehot_dest * jnp.arange(samp_count)[None, :], axis=1)
    tail = source.shape[0] - 2 * row_count
    target_at = jnp.concatenate([target, target, jnp.full((tail,), -1, jnp.int32)])
    slot_at = jnp.concatenate([slot_index, jnp.full((source.shape[0] - row_count,), -1, jnp.int32)])
    d_i = jnp.arange(samp_count)[:, None, None]
    r_i = jnp.arange(slot_cap + 4)[None, :, None]
    s_i = jnp.arange(source.shape[0])[None, None, :]
    to_dest = d_i == target_at[None, None, :]
    pick = (
        (to_dest & (r_i == slot_at[None, None, :]))
        | (to_dest & (r_i == slot_cap) & (s_i >= row_count))
        | ((r_i == slot_cap + 1) & (s_i < row_count))
    )
    wide = jnp.einsum(
        "dri,if->drf", pick.astype(jnp.bfloat16), source, preferred_element_type=jnp.float32
    )
    col_sums = wide[:, slot_cap + 1, :]
    col_lo = col_sums - lax.reduce_precision(col_sums, exponent_bits=8, mantissa_bits=7)
    packet = jnp.where(r_i[0] == slot_cap + 2, col_lo[:, None, :], wide).astype(jnp.bfloat16)
    got = lax.all_to_all(packet, SAMP, split_axis=0, concat_axis=0, tiled=True)
    flat_rows = got[:, :slot_cap, :].reshape(-1, feat_width)
    flat_ids = got[:, slot_cap, :slot_cap].reshape(-1).astype(jnp.int32) - 1
    grand_total = jnp.sum(
        got[:, slot_cap + 1, :].astype(jnp.float32) + got[:, slot_cap + 2, :].astype(jnp.float32),
        axis=0,
    )
    member = jnp.arange(class_cap)[:, None] == flat_ids[None, :]
    class_sums = jnp.dot(member.astype(jnp.bfloat16), flat_rows, preferred_element_type=jnp.float32)
    counts = jnp.sum(member.astype(jnp.float32), axis=1)
    class_means = class_sums / jnp.maximum(counts, 1.0)[:, None]
    center = grand_total / (row_count * samp_count)
    is_valid = flat_ids >= 0
    hi_part = lax.reduce_precision(class_means, exponent_bits=8, mantissa_bits=7)
    rest = class_means - hi_part
    mid_part = lax.reduce_precision(rest, exponent_bits=8, mantissa_bits=7)
    mean_hi = hi_part.astype(jnp.bfloat16)
    mean_mid = mid_part.astype(jnp.bfloat16)
    mean_lo = (rest - mid_part).astype(jnp.bfloat16)
    lookup = member.T.astype(jnp.bfloat16)
    picked = (
        jnp.dot(lookup, mean_hi, preferred_element_type=jnp.float32)
        + jnp.dot(lookup, mean_mid, preferred_element_type=jnp.float32)
    ) + jnp.dot(lookup, mean_lo, preferred_element_type=jnp.float32)
    centred = jnp.where(is_valid[:, None], flat_rows.astype(jnp.float32) - picked, 0.0).astype(
        jnp.bfloat16
    )
    deviation = (class_means - center[None, :]).astype(jnp.bfloat16)
    part_within = jnp.dot(centred, basis, preferred_element_type=jnp.float32)
    part_between = jnp.dot(deviation, basis, preferred_element_type=jnp.float32)
    parts = jnp.concatenate([part_within, part_between], axis=0).astype(jnp.bfloat16)
    n_rows = parts.shape[0]
    chunk = n_rows // feat_count
    swapped = lax.all_to_all(
        parts.reshape(feat_count, chunk, k_width), "feat", split_axis=0, concat_axis=0, tiled=True
    )
    copies = jnp.einsum(
        "jcn,jd->dcn", swapped, jnp.ones((feat_count, feat_count), jnp.bfloat16),
        preferred_element_type=jnp.float32,
    ).astype(jnp.bfloat16)
    spread = lax.all_to_all(
        copies,
        "feat",
        split_axis=0,
        concat_axis=0,
        tiled=True,
    ).reshape(n_rows, k_width)
    n_within = part_within.shape[0]
    projected = spread[:n_within]
    weighted = (counts[:, None] * spread[n_within:].astype(jnp.float32)).astype(jnp.bfloat16)
    contract = (((0,), (0,)), ((), ()))
    term_within = lax.dot_general(projected, centred, contract, preferred_element_type=jnp.float32)
    term_between = lax.dot_general(
        weighted, deviation, contract, preferred_element_type=jnp.float32
    )
    k_share = k_width // samp_count
    core_count = lax.axis_size("core")
    chip_count = samp_count // core_count
    both = jnp.stack([term_within, term_between]).reshape(
        2, chip_count, core_count, k_share, feat_width
    )
    pair = lax.all_to_all(
        both.astype(jnp.bfloat16), "core", split_axis=2, concat_axis=2, tiled=True
    )
    per_chip = jnp.sum(pair.astype(jnp.float32), axis=2).astype(jnp.bfloat16)
    swapped = lax.all_to_all(per_chip, "chip", split_axis=1, concat_axis=1, tiled=True)
    summed = jnp.sum(swapped.astype(jnp.float32), axis=1)
    within, between = summed[0], summed[1]
    inv_count = 1.0 / (row_count * samp_count)
    return (class_means.astype(jnp.bfloat16), within * inv_count, between * inv_count)


def solution(mesh):
    samp_size = mesh.shape["samp"]
    split = jax.sharding.Mesh(
        mesh.devices.reshape(samp_size // 2, 2, mesh.shape["feat"]), ("chip", "core", "feat")
    )
    in_specs = (P(SAMP, "feat"), P(SAMP), P(), P("feat", None))
    out_specs = (P(SAMP, "feat"), P(SAMP, "feat"), P(SAMP, "feat"))
    return jax.shard_map(
        on_device, mesh=split, in_specs=in_specs, out_specs=out_specs, check_vma=False
    )
```

```python
import jax
import jax.numpy as jnp
from jax import lax
from jax.sharding import PartitionSpec as P

CLS_DEV = 192
SAMP = ("chip", "core")


def on_device(images, labels, owner, basis):
    samp_count = lax.axis_size(SAMP)
    feat_count = lax.axis_size("feat")
    row_count, feat_width = images.shape
    slot_cap = 2 * row_count // samp_count
    class_cap = CLS_DEV
    class_total = owner.shape[0]
    k_width = basis.shape[1]
    owner_table = (owner[:, None] == jnp.arange(samp_count)[None, :]).astype(jnp.bfloat16)
    class_ids = jnp.arange(class_total)[None, :]
    marks = (class_ids < labels[:, None]).astype(jnp.bfloat16) + 256.0 * (
        class_ids == labels[:, None]
    ).astype(jnp.bfloat16)
    tallies = jnp.dot(marks, owner_table, preferred_element_type=jnp.float32)
    dest_hot = (tallies >= 256.0).astype(jnp.float32)
    below = tallies - 256.0 * dest_hot
    slot_ids = jnp.sum(below * dest_hot, axis=1)
    onehot_dest = dest_hot.astype(jnp.int32)
    slot_index = jnp.sum(jnp.cumsum(onehot_dest, axis=0) * onehot_dest, axis=1) - 1
    slot_hot = (slot_index[:, None] == jnp.arange(slot_cap)[None, :]).astype(jnp.float32)
    lane = jnp.arange(feat_width)[None, :]
    id_rows = (
        (lane == slot_index[:, None]).astype(jnp.float32) * (slot_ids + 1.0)[:, None]
    ).astype(jnp.bfloat16)
    source = jnp.concatenate([images, id_rows], axis=0)
    target = jnp.sum(onehot_dest * jnp.arange(samp_count)[None, :], axis=1)
    tail = source.shape[0] - 2 * row_count
    target_at = jnp.concatenate([target, target, jnp.full((tail,), -1, jnp.int32)])
    slot_at = jnp.concatenate([slot_index, jnp.full((source.shape[0] - row_count,), -1, jnp.int32)])
    d_i = jnp.arange(samp_count)[:, None, None]
    r_i = jnp.arange(slot_cap + 3)[None, :, None]
    s_i = jnp.arange(source.shape[0])[None, None, :]
    to_dest = d_i == target_at[None, None, :]
    pick = (
        (to_dest & (r_i == slot_at[None, None, :]))
        | (to_dest & (r_i == slot_cap) & (s_i >= row_count))
        | ((r_i == slot_cap + 1) & (s_i < row_count))
    )
    wide = jnp.einsum(
        "dri,if->drf", pick.astype(jnp.bfloat16), source, preferred_element_type=jnp.float32
    )
    col_sums = wide[:, slot_cap + 1, :]
    col_lo = col_sums - lax.reduce_precision(col_sums, exponent_bits=8, mantissa_bits=7)
    packet = jnp.where(r_i[0] == slot_cap + 2, col_lo[:, None, :], wide).astype(jnp.bfloat16)
    got = lax.all_to_all(packet, SAMP, split_axis=0, concat_axis=0, tiled=True)
    flat_rows = got[:, :slot_cap, :].reshape(-1, feat_width)
    flat_ids = got[:, slot_cap, :slot_cap].reshape(-1).astype(jnp.int32) - 1
    grand_total = jnp.sum(
        got[:, slot_cap + 1, :].astype(jnp.float32) + got[:, slot_cap + 2, :].astype(jnp.float32),
        axis=0,
    )
    member = jnp.arange(class_cap)[:, None] == flat_ids[None, :]
    class_sums = jnp.dot(member.astype(jnp.bfloat16), flat_rows, preferred_element_type=jnp.float32)
    counts = jnp.sum(member.astype(jnp.float32), axis=1)
    class_means = class_sums / jnp.maximum(counts, 1.0)[:, None]
    center = grand_total / (row_count * samp_count)
    is_valid = flat_ids >= 0
    hi_part = lax.reduce_precision(class_means, exponent_bits=8, mantissa_bits=7)
    rest = class_means - hi_part
    mid_part = lax.reduce_precision(rest, exponent_bits=8, mantissa_bits=7)
    mean_hi = hi_part.astype(jnp.bfloat16)
    mean_mid = mid_part.astype(jnp.bfloat16)
    mean_lo = (rest - mid_part).astype(jnp.bfloat16)
    lookup = member.T.astype(jnp.bfloat16)
    picked = (
        jnp.dot(lookup, mean_hi, preferred_element_type=jnp.float32)
        + jnp.dot(lookup, mean_mid, preferred_element_type=jnp.float32)
    ) + jnp.dot(lookup, mean_lo, preferred_element_type=jnp.float32)
    centred = jnp.where(is_valid[:, None], flat_rows.astype(jnp.float32) - picked, 0.0).astype(
        jnp.bfloat16
    )
    deviation = (class_means - center[None, :]).astype(jnp.bfloat16)
    part_within = jnp.dot(centred, basis, preferred_element_type=jnp.float32)
    part_between = jnp.dot(deviation, basis, preferred_element_type=jnp.float32)
    parts = jnp.concatenate([part_within, part_between], axis=0).astype(jnp.bfloat16)
    n_rows = parts.shape[0]
    chunk = n_rows // feat_count
    swapped = lax.all_to_all(
        parts.reshape(feat_count, chunk, k_width), "feat", split_axis=0, concat_axis=0, tiled=True
    )
    copies = jnp.einsum(
        "jcn,jd->dcn", swapped, jnp.ones((feat_count, feat_count), jnp.bfloat16),
        preferred_element_type=jnp.float32,
    ).astype(jnp.bfloat16)
    spread = lax.all_to_all(
        copies,
        "feat",
        split_axis=0,
        concat_axis=0,
        tiled=True,
    ).reshape(n_rows, k_width)
    n_within = part_within.shape[0]
    projected = spread[:n_within]
    weighted = (counts[:, None] * spread[n_within:].astype(jnp.float32)).astype(jnp.bfloat16)
    contract = (((0,), (0,)), ((), ()))
    term_within = lax.dot_general(projected, centred, contract, preferred_element_type=jnp.float32)
    term_between = lax.dot_general(
        weighted, deviation, contract, preferred_element_type=jnp.float32
    )
    k_share = k_width // samp_count
    core_count = lax.axis_size("core")
    chip_count = samp_count // core_count
    both = jnp.stack([term_within, term_between]).reshape(
        2, chip_count, core_count, k_share, feat_width
    )
    pair = lax.all_to_all(
        both.astype(jnp.bfloat16), "core", split_axis=2, concat_axis=2, tiled=True
    )
    per_chip = jnp.sum(pair.astype(jnp.float32), axis=2).astype(jnp.bfloat16)
    swapped = lax.all_to_all(per_chip, "chip", split_axis=1, concat_axis=1, tiled=True)
    summed = jnp.sum(swapped.astype(jnp.float32), axis=1)
    within, between = summed[0], summed[1]
    inv_count = 1.0 / (row_count * samp_count)
    return (class_means.astype(jnp.bfloat16), within * inv_count, between * inv_count)


def solution(mesh):
    samp_size = mesh.shape["samp"]
    split = jax.sharding.Mesh(
        mesh.devices.reshape(samp_size // 2, 2, mesh.shape["feat"]), ("chip", "core", "feat")
    )
    in_specs = (P(SAMP, "feat"), P(SAMP), P(), P("feat", None))
    out_specs = (P(SAMP, "feat"), P(SAMP, "feat"), P(SAMP, "feat"))
    return jax.shard_map(
        on_device, mesh=split, in_specs=in_specs, out_specs=out_specs, check_vma=False
    )
```

```python
import jax
import jax.numpy as jnp
from jax import lax
from jax.sharding import PartitionSpec as P

CLS_DEV = 192
SAMP = ("chip", "core")


def on_device(images, labels, owner, basis):
    samp_count = lax.axis_size(SAMP)
    feat_count = lax.axis_size("feat")
    row_count, feat_width = images.shape
    slot_cap = 2 * row_count // samp_count
    class_cap = CLS_DEV
    class_total = owner.shape[0]
    k_width = basis.shape[1]
    owner_table = (owner[:, None] == jnp.arange(samp_count)[None, :]).astype(jnp.bfloat16)
    class_ids = jnp.arange(class_total)[None, :]
    marks = (class_ids < labels[:, None]).astype(jnp.bfloat16) + 256.0 * (
        class_ids == labels[:, None]
    ).astype(jnp.bfloat16)
    tallies = jnp.dot(marks, owner_table, preferred_element_type=jnp.float32)
    dest_hot = (tallies >= 256.0).astype(jnp.float32)
    below = tallies - 256.0 * dest_hot
    slot_ids = jnp.sum(below * dest_hot, axis=1)
    onehot_dest = dest_hot.astype(jnp.int32)
    slot_index = jnp.sum(jnp.cumsum(onehot_dest, axis=0) * onehot_dest, axis=1) - 1
    slot_hot = (slot_index[:, None] == jnp.arange(slot_cap)[None, :]).astype(jnp.float32)
    lane = jnp.arange(feat_width)[None, :]
    id_rows = (
        (lane == slot_index[:, None]).astype(jnp.float32) * (slot_ids + 1.0)[:, None]
    ).astype(jnp.bfloat16)
    source = jnp.concatenate([images, id_rows], axis=0)
    target = jnp.sum(onehot_dest * jnp.arange(samp_count)[None, :], axis=1)
    tail = source.shape[0] - 2 * row_count
    target_at = jnp.concatenate([target, target, jnp.full((tail,), -1, jnp.int32)])
    slot_at = jnp.concatenate([slot_index, jnp.full((source.shape[0] - row_count,), -1, jnp.int32)])
    d_i = jnp.arange(samp_count)[:, None, None]
    r_i = jnp.arange(slot_cap + 4)[None, :, None]
    s_i = jnp.arange(source.shape[0])[None, None, :]
    to_dest = d_i == target_at[None, None, :]
    pick = (
        (to_dest & (r_i == slot_at[None, None, :]))
        | (to_dest & (r_i == slot_cap) & (s_i >= row_count))
        | ((r_i == slot_cap + 1) & (s_i < row_count))
    )
    wide = jnp.einsum(
        "dri,if->drf", pick.astype(jnp.bfloat16), source, preferred_element_type=jnp.float32
    )
    col_sums = wide[:, slot_cap + 1, :]
    col_lo = col_sums - lax.reduce_precision(col_sums, exponent_bits=8, mantissa_bits=7)
    packet = jnp.where(r_i[0] == slot_cap + 2, col_lo[:, None, :], wide).astype(jnp.bfloat16)
    got = lax.all_to_all(packet, SAMP, split_axis=0, concat_axis=0, tiled=True)
    flat_rows = got[:, :slot_cap, :].reshape(-1, feat_width)
    flat_ids = got[:, slot_cap, :slot_cap].reshape(-1).astype(jnp.int32) - 1
    grand_total = jnp.sum(
        got[:, slot_cap + 1, :].astype(jnp.float32) + got[:, slot_cap + 2, :].astype(jnp.float32),
        axis=0,
    )
    member = jnp.arange(class_cap)[:, None] == flat_ids[None, :]
    class_sums = jnp.dot(member.astype(jnp.bfloat16), flat_rows, preferred_element_type=jnp.float32)
    counts = jnp.sum(member.astype(jnp.float32), axis=1)
    class_means = class_sums / jnp.maximum(counts, 1.0)[:, None]
    center = grand_total / (row_count * samp_count)
    is_valid = flat_ids >= 0
    hi_part = lax.reduce_precision(class_means, exponent_bits=8, mantissa_bits=7)
    rest = class_means - hi_part
    mid_part = lax.reduce_precision(rest, exponent_bits=8, mantissa_bits=7)
    mean_hi = hi_part.astype(jnp.bfloat16)
    mean_mid = mid_part.astype(jnp.bfloat16)
    mean_lo = (rest - mid_part).astype(jnp.bfloat16)
    lookup = member.T.astype(jnp.bfloat16)
    picked = (
        jnp.dot(lookup, mean_hi, preferred_element_type=jnp.float32)
        + jnp.dot(lookup, mean_mid, preferred_element_type=jnp.float32)
    ) + jnp.dot(lookup, mean_lo, preferred_element_type=jnp.float32)
    centred = jnp.where(is_valid[:, None], flat_rows.astype(jnp.float32) - picked, 0.0).astype(
        jnp.bfloat16
    )
    deviation = (class_means - center[None, :]).astype(jnp.bfloat16)
    part_within = jnp.dot(centred, basis, preferred_element_type=jnp.float32)
    part_between = jnp.dot(deviation, basis, preferred_element_type=jnp.float32)
    parts = jnp.concatenate([part_within, part_between], axis=0).astype(jnp.bfloat16)
    n_rows = parts.shape[0]
    chunk = n_rows // feat_count
    swapped = lax.all_to_all(
        parts.reshape(feat_count, chunk, k_width), "feat", split_axis=0, concat_axis=0, tiled=True
    )
    copies = jnp.einsum(
        "jcn,jd->dcn", swapped, jnp.ones((feat_count, feat_count), jnp.bfloat16),
        preferred_element_type=jnp.float32,
    ).astype(jnp.bfloat16)
    spread = lax.all_to_all(
        copies,
        "feat",
        split_axis=0,
        concat_axis=0,
        tiled=True,
    ).reshape(n_rows, k_width)
    n_within = part_within.shape[0]
    projected = spread[:n_within]
    weighted = (counts[:, None] * spread[n_within:].astype(jnp.float32)).astype(jnp.bfloat16)
    contract = (((0,), (0,)), ((), ()))
    term_within = lax.dot_general(projected, centred, contract, preferred_element_type=jnp.float32)
    term_between = lax.dot_general(
        weighted, deviation, contract, preferred_element_type=jnp.float32
    )
    k_share = k_width // samp_count
    core_count = lax.axis_size("core")
    chip_count = samp_count // core_count
    both = jnp.stack([term_within, term_between]).reshape(
        2, chip_count, core_count, k_share, feat_width
    )
    core = lax.axis_index("core")
    halves = both.astype(jnp.bfloat16)
    mine = lax.dynamic_index_in_dim(halves, core, axis=2, keepdims=False)
    theirs = lax.dynamic_index_in_dim(halves, 1 - core, axis=2, keepdims=False)
    got_half = lax.ppermute(theirs, "core", [(0, 1), (1, 0)])
    per_chip = (mine.astype(jnp.float32) + got_half.astype(jnp.float32)).astype(jnp.bfloat16)
    swapped = lax.all_to_all(per_chip, "chip", split_axis=1, concat_axis=1, tiled=True)
    summed = jnp.sum(swapped.astype(jnp.float32), axis=1)
    within, between = summed[0], summed[1]
    inv_count = 1.0 / (row_count * samp_count)
    return (class_means.astype(jnp.bfloat16), within * inv_count, between * inv_count)


def solution(mesh):
    samp_size = mesh.shape["samp"]
    split = jax.sharding.Mesh(
        mesh.devices.reshape(samp_size // 2, 2, mesh.shape["feat"]), ("chip", "core", "feat")
    )
    in_specs = (P(SAMP, "feat"), P(SAMP), P(), P("feat", None))
    out_specs = (P(SAMP, "feat"), P(SAMP, "feat"), P(SAMP, "feat"))
    return jax.shard_map(
        on_device, mesh=split, in_specs=in_specs, out_specs=out_specs, check_vma=False
    )
```

```python
import jax
import jax.numpy as jnp
from jax import lax
from jax.sharding import PartitionSpec as P

CLS_DEV = 192
SAMP = ("chip", "core")


def on_device(images, labels, owner, basis):
    samp_count = lax.axis_size(SAMP)
    feat_count = lax.axis_size("feat")
    row_count, feat_width = images.shape
    slot_cap = 2 * row_count // samp_count
    class_cap = CLS_DEV
    class_total = owner.shape[0]
    k_width = basis.shape[1]
    owner_rows = (jnp.arange(samp_count)[:, None] == owner[None, :]).astype(jnp.bfloat16)
    class_ids = jnp.arange(class_total)[None, :]
    marks = (class_ids < labels[:, None]).astype(jnp.bfloat16) + 256.0 * (
        class_ids == labels[:, None]
    ).astype(jnp.bfloat16)
    tallies = lax.dot_general(
        marks, owner_rows, (((1,), (1,)), ((), ())), preferred_element_type=jnp.float32
    )
    dest_hot = (tallies >= 256.0).astype(jnp.float32)
    below = tallies - 256.0 * dest_hot
    slot_ids = jnp.sum(below * dest_hot, axis=1)
    onehot_dest = dest_hot.astype(jnp.int32)
    slot_index = jnp.sum(jnp.cumsum(onehot_dest, axis=0) * onehot_dest, axis=1) - 1
    slot_hot = (slot_index[:, None] == jnp.arange(slot_cap)[None, :]).astype(jnp.float32)
    lane = jnp.arange(feat_width)[None, :]
    id_rows = (
        (lane == slot_index[:, None]).astype(jnp.float32) * (slot_ids + 1.0)[:, None]
    ).astype(jnp.bfloat16)
    source = jnp.concatenate([images, id_rows], axis=0)
    target = jnp.sum(onehot_dest * jnp.arange(samp_count)[None, :], axis=1)
    tail = source.shape[0] - 2 * row_count
    target_at = jnp.concatenate([target, target, jnp.full((tail,), -1, jnp.int32)])
    slot_at = jnp.concatenate([slot_index, jnp.full((source.shape[0] - row_count,), -1, jnp.int32)])
    d_i = jnp.arange(samp_count)[:, None, None]
    r_i = jnp.arange(slot_cap + 4)[None, :, None]
    s_i = jnp.arange(source.shape[0])[None, None, :]
    to_dest = d_i == target_at[None, None, :]
    pick = (
        (to_dest & (r_i == slot_at[None, None, :]))
        | (to_dest & (r_i == slot_cap) & (s_i >= row_count))
        | ((r_i == slot_cap + 1) & (s_i < row_count))
    )
    wide = jnp.einsum(
        "dri,if->drf", pick.astype(jnp.bfloat16), source, preferred_element_type=jnp.float32
    )
    col_sums = wide[:, slot_cap + 1, :]
    col_lo = col_sums - lax.reduce_precision(col_sums, exponent_bits=8, mantissa_bits=7)
    packet = jnp.where(r_i[0] == slot_cap + 2, col_lo[:, None, :], wide).astype(jnp.bfloat16)
    got = lax.all_to_all(packet, SAMP, split_axis=0, concat_axis=0, tiled=True)
    flat_rows = got[:, :slot_cap, :].reshape(-1, feat_width)
    flat_ids = got[:, slot_cap, :slot_cap].reshape(-1).astype(jnp.int32) - 1
    grand_total = jnp.sum(
        got[:, slot_cap + 1, :].astype(jnp.float32) + got[:, slot_cap + 2, :].astype(jnp.float32),
        axis=0,
    )
    member = jnp.arange(class_cap)[:, None] == flat_ids[None, :]
    class_sums = jnp.dot(member.astype(jnp.bfloat16), flat_rows, preferred_element_type=jnp.float32)
    counts = jnp.sum(member.astype(jnp.float32), axis=1)
    class_means = class_sums / jnp.maximum(counts, 1.0)[:, None]
    center = grand_total / (row_count * samp_count)
    is_valid = flat_ids >= 0
    hi_part = lax.reduce_precision(class_means, exponent_bits=8, mantissa_bits=7)
    rest = class_means - hi_part
    mid_part = lax.reduce_precision(rest, exponent_bits=8, mantissa_bits=7)
    mean_hi = hi_part.astype(jnp.bfloat16)
    mean_mid = mid_part.astype(jnp.bfloat16)
    mean_lo = (rest - mid_part).astype(jnp.bfloat16)
    lookup = member.T.astype(jnp.bfloat16)
    picked = (
        jnp.dot(lookup, mean_hi, preferred_element_type=jnp.float32)
        + jnp.dot(lookup, mean_mid, preferred_element_type=jnp.float32)
    ) + jnp.dot(lookup, mean_lo, preferred_element_type=jnp.float32)
    centred = jnp.where(is_valid[:, None], flat_rows.astype(jnp.float32) - picked, 0.0).astype(
        jnp.bfloat16
    )
    deviation = (class_means - center[None, :]).astype(jnp.bfloat16)
    part_within = jnp.dot(centred, basis, preferred_element_type=jnp.float32)
    part_between = jnp.dot(deviation, basis, preferred_element_type=jnp.float32)
    parts = jnp.concatenate([part_within, part_between], axis=0).astype(jnp.bfloat16)
    n_rows = parts.shape[0]
    chunk = n_rows // feat_count
    swapped = lax.all_to_all(
        parts.reshape(feat_count, chunk, k_width), "feat", split_axis=0, concat_axis=0, tiled=True
    )
    copies = jnp.einsum(
        "jcn,jd->dcn", swapped, jnp.ones((feat_count, feat_count), jnp.bfloat16),
        preferred_element_type=jnp.float32,
    ).astype(jnp.bfloat16)
    spread = lax.all_to_all(
        copies,
        "feat",
        split_axis=0,
        concat_axis=0,
        tiled=True,
    ).reshape(n_rows, k_width)
    n_within = part_within.shape[0]
    projected = spread[:n_within]
    weighted = (counts[:, None] * spread[n_within:].astype(jnp.float32)).astype(jnp.bfloat16)
    contract = (((0,), (0,)), ((), ()))
    term_within = lax.dot_general(projected, centred, contract, preferred_element_type=jnp.float32)
    term_between = lax.dot_general(
        weighted, deviation, contract, preferred_element_type=jnp.float32
    )
    k_share = k_width // samp_count
    core_count = lax.axis_size("core")
    chip_count = samp_count // core_count
    both = jnp.stack([term_within, term_between]).reshape(
        2, chip_count, core_count, k_share, feat_width
    )
    pair = lax.all_to_all(
        both.astype(jnp.bfloat16), "core", split_axis=2, concat_axis=2, tiled=True
    )
    per_chip = jnp.sum(pair.astype(jnp.float32), axis=2).astype(jnp.bfloat16)
    swapped = lax.all_to_all(per_chip, "chip", split_axis=1, concat_axis=1, tiled=True)
    summed = jnp.sum(swapped.astype(jnp.float32), axis=1)
    within, between = summed[0], summed[1]
    inv_count = 1.0 / (row_count * samp_count)
    return (class_means.astype(jnp.bfloat16), within * inv_count, between * inv_count)


def solution(mesh):
    samp_size = mesh.shape["samp"]
    split = jax.sharding.Mesh(
        mesh.devices.reshape(samp_size // 2, 2, mesh.shape["feat"]), ("chip", "core", "feat")
    )
    in_specs = (P(SAMP, "feat"), P(SAMP), P(), P("feat", None))
    out_specs = (P(SAMP, "feat"), P(SAMP, "feat"), P(SAMP, "feat"))
    return jax.shard_map(
        on_device, mesh=split, in_specs=in_specs, out_specs=out_specs, check_vma=False
    )
```
